512 devices in a mesh: seq: 64 (over x, z, y_lo), head: 8 (over y_hi, core).
Axes of the slice: x: 4, y: 8 (y_hi: 4, y_lo: 2; y = y_hi * 2 + y_lo), z: 8, core: 2. Of those that a mesh axis runs over, the one named last changes fastest.
Arguments:
- queries: bfloat16 [8192, 8192], P('seq', 'head'), may hold values from -14 to 14, as said below
- key_tokens: bfloat16 [8192, 1024], P(('seq', 'head')), may hold values from -6 to 6, as said below
- value_tokens: bfloat16 [8192, 1024], P(('seq', 'head')), may hold values from -6 to 6
- key_scales: bfloat16 [128, 8], P('seq', 'head'), may hold values from 0.25 to 2.5
- value_scales: bfloat16 [128, 8], P('seq', 'head'), may hold values from 0.25 to 2.5
- value_means: float32 [1024], P('head'), may hold values from -4 to 4
- doc_lengths: int32 [64], replicated, may hold values from 1 to 5120, 8192 in all
Outputs:
- attended: bfloat16 [8192, 8192], P('seq', 'head')
The draws below stay inside these ranges and needn't reach their ends.
Inputs may be any that keep to these rules, and one draw needn't show every extreme that they name: `doc_lengths`: positive lengths of the documents in order; they sum to 8192, and the longest has exactly 5120 tokens. `queries`: finite values. `key_tokens`: finite values.
All inputs are finite; a program needn't handle non-finite values.
Results may differ from the reference program's by a relative error of at most 0.002.
Values may be sent and summed in bfloat16 or wider, within the bound.
No kernel may reach another device: no remote copies, remote signals or barrier semaphores. Data moves between devices by JAX's collectives and lax.ppermute only.
A program may use at most 64 MiB of HBM per device.

```python
import math
import jax
import jax.numpy as jnp
import numpy as np
from jax import lax

QH = 64
KVH = 8
HD = 128
BLK = 64
DOCS = 64
TOKENS = 8192
MOST = 5120


def shared_keys(key):
    base_key = jax.random.fold_in(key, 11)
    raw_values = jnp.clip(jax.random.normal(base_key, (TOKENS, KVH, HD), jnp.float32), -6.0, 6.0)
    return raw_values


def draw_key_tokens(key, part):
    return shared_keys(key).reshape(TOKENS, KVH * HD).astype(jnp.bfloat16)


def draw_queries(key, part):
    group_size = QH // KVH
    base_key = jax.random.fold_in(key, 23)
    raw_values = jnp.clip(jax.random.normal(base_key, (TOKENS, KVH, group_size, HD), jnp.float32), -6.0, 6.0)
    return raw_values.reshape(TOKENS, QH * HD).astype(jnp.bfloat16)


def level_of(stream_key, shape, shards, least, top_value):
    loudness, own = 1.0, jax.random.fold_in(stream_key, 6)
    for dim, blocks in shards:
        heights = jnp.exp(jax.random.uniform(jax.random.fold_in(own, dim), (blocks,), jnp.float32, least / len(shards), top_value / len(shards)))
        loudness = loudness * jnp.repeat(heights, shape[dim] // blocks).reshape([-1 if axis == dim else 1 for axis in range(len(shape))])
    return loudness


def profile(number_of, total, reach, lean):
    portions = [(1 << 20) // math.isqrt(grade ** lean) + 1 for grade in range(2, number_of + 1)]
    rest, given = total - reach - (number_of - 1), [1] * (number_of - 1)
    while rest > 0:
        movable = [i for i in range(number_of - 1) if given[i] < reach]
        mass, left = sum([portions[i] for i in movable]), rest
        for i in movable:
            more = min(reach - given[i], max(1, left * portions[i] // mass), rest)
            given[i] = given[i] + more
            rest = rest - more
    return np.array([reach] + given)


def ragged(stream_key, count, total, reach, slope):
    if count == 2:
        one = jax.random.randint(stream_key, (), max(1, total - reach), min(reach, total - 1) + 1)
        return jnp.stack([one, total - one])
    lengths = jnp.asarray(profile(count, total, reach, slope), jnp.int32)
    pairs = (count - 1) // 2
    giver, taker = lengths[1:1 + 2 * pairs:2], lengths[2:2 + 2 * pairs:2]
    margin = jnp.minimum(giver - 1, reach - taker)
    shifted = jax.random.randint(jax.random.fold_in(stream_key, 1), (pairs,), 0, 1 << 20) % (margin + 1)
    lengths = lengths.at[1:1 + 2 * pairs:2].set(giver - shifted).at[2:2 + 2 * pairs:2].set(taker + shifted)
    return lengths[jax.random.permutation(jax.random.fold_in(stream_key, 2), count)]


def centred(own_key, shape, width, most, pieces=(), kind=jnp.bfloat16):
    loudness = level_of(own_key, shape, pieces, -0.22, 0.18) if pieces else 1.0
    values = jax.random.normal(own_key, shape, jnp.float32) * width * loudness
    return jnp.minimum(jnp.maximum(values, -most), most).astype(kind)


def setup_inputs(seed: int = 0) -> dict:
    splits = jax.random.split(jax.random.key(seed), 8)
    return {
        "queries": draw_queries(jax.random.fold_in(splits[7], 71), 0),
        "key_tokens": draw_key_tokens(jax.random.fold_in(splits[7], 71), 0),
        "value_tokens": centred(splits[2], (TOKENS, KVH * HD), 1.0, 6.0, ((0, 512),)),
        "key_scales": jnp.clip(jnp.exp(math.log(2.5) - 2.3025851 * jax.random.uniform(splits[3], (TOKENS // BLK, KVH), jnp.float32) ** level_of(splits[3], (TOKENS // BLK, KVH), ((0, 64), (1, 8)), -0.2, 0.2)), 0.25, 2.5).astype(jnp.bfloat16),
        "value_scales": jnp.clip(jnp.exp(math.log(2.5) - 2.3025851 * jax.random.uniform(splits[4], (TOKENS // BLK, KVH), jnp.float32) ** level_of(splits[4], (TOKENS // BLK, KVH), ((0, 64), (1, 8)), -0.2, 0.2)), 0.25, 2.5).astype(jnp.bfloat16),
        "value_means": centred(splits[5], (KVH * HD,), 1.0, 4.0, ((0, 8),), jnp.float32),
        "doc_lengths": ragged(splits[6], DOCS, TOKENS, MOST, 1).astype(jnp.int32),
    }


NEG = -1e+30

def reference(queries, key_tokens, value_tokens, key_scales, value_scales, value_means, doc_lengths):
    token_count = queries.shape[0]
    group_size = QH // KVH
    inv_scale = 1.0 / math.sqrt(HD)
    starts = jnp.cumsum(doc_lengths) - doc_lengths
    positions = jnp.arange(token_count, dtype=jnp.int32)
    docs = lax.optimization_barrier(jnp.sum((starts[None, :] <= positions[:, None]).astype(jnp.int32), axis=1)) - 1
    query_block = math.gcd(token_count, 128)
    window = min(MOST + query_block, token_count)
    key_heads = key_tokens.reshape(token_count, KVH, HD)
    value_heads = value_tokens.reshape(token_count, KVH, HD)
    key_scale_rows = jnp.repeat(key_scales.astype(jnp.float32), BLK, axis=0)
    value_scale_rows = jnp.repeat(value_scales.astype(jnp.float32), BLK, axis=0)
    query_heads = queries.reshape(token_count, KVH, group_size, HD)
    mean_rows = value_means.reshape(KVH, 1, 1, HD)

    def one_block(first_query):
        first_key = jnp.clip(first_query + query_block - window, 0, token_count - window).astype(jnp.int32)
        query_tile = lax.dynamic_slice_in_dim(query_heads, first_query, query_block, 0).astype(jnp.float32)
        key_tile = lax.dynamic_slice_in_dim(key_heads, first_key, window, 0).astype(jnp.float32)
        value_tile = lax.dynamic_slice_in_dim(value_heads, first_key, window, 0).astype(jnp.float32)
        key_scale_tile = lax.dynamic_slice_in_dim(key_scale_rows, first_key, window, 0)
        value_scale_tile = lax.dynamic_slice_in_dim(value_scale_rows, first_key, window, 0)
        query_pos = first_query + jnp.arange(query_block, dtype=jnp.int32)
        key_pos = first_key + jnp.arange(window, dtype=jnp.int32)
        query_doc = lax.dynamic_slice_in_dim(docs, first_query, query_block, 0)
        key_doc = lax.dynamic_slice_in_dim(docs, first_key, window, 0)
        allowed = (key_doc[None, :] == query_doc[:, None]) & (key_pos[None, :] <= query_pos[:, None])
        scores = jnp.einsum('rkgd,nkd->kgrn', query_tile, key_tile)
        scores = scores * (key_scale_tile.T * inv_scale)[:, None, None, :]
        scores = jnp.where(allowed[None, None], scores, NEG)
        peak = lax.optimization_barrier(jnp.max(scores, axis=-1))
        weights = jnp.where(allowed[None, None], jnp.exp(scores - peak[..., None]), 0.0)
        total = lax.optimization_barrier(jnp.sum(weights, axis=-1))
        scaled = (weights * value_scale_tile.T[:, None, None, :]).astype(jnp.bfloat16)
        scaled = lax.optimization_barrier(scaled).astype(jnp.float32)
        mixture = jnp.einsum('kgrn,nkd->kgrd', scaled, value_tile)
        result = mixture / total[..., None] + mean_rows
        return result.transpose(2, 0, 1, 3).reshape(query_block, QH * HD).astype(jnp.bfloat16)
    firsts = jnp.arange(token_count // query_block, dtype=jnp.int32) * query_block
    blocks_out = lax.map(one_block, firsts)
    return blocks_out.reshape(token_count, QH * HD)
```

```python
import math

import jax
import jax.numpy as jnp
from jax import lax
from jax.sharding import PartitionSpec as P

QH = 64
KVH = 8
HD = 128
BLK = 64
MOST = 5120


NEG = -1e30


def doc_index(positions, starts):
    return jnp.sum((starts[None, :] <= positions[:, None]).astype(jnp.int32), axis=1) - 1


def block_update(
    totals,
    query_tile,
    query_pos,
    query_doc,
    key_tile,
    value_tile,
    key_scale,
    value_scale,
    key_pos,
    starts,
):
    inv_scale = 1.0 / math.sqrt(HD)
    key_doc = doc_index(key_pos, starts)
    allowed = (key_doc[None, :] == query_doc[:, None]) & (key_pos[None, :] <= query_pos[:, None])

    def update(current):
        run_max, run_sum, accumulate = current
        scores = jnp.einsum(
            "kgrd,nkd->kgrn", query_tile, key_tile, preferred_element_type=jnp.float32
        )
        scores = scores * (key_scale.T * inv_scale)[:, None, None, :]
        scores = jnp.where(allowed[None, None], scores, NEG)
        new_max = jnp.maximum(run_max, jnp.max(scores, axis=-1))
        weights = jnp.where(allowed[None, None], jnp.exp(scores - new_max[..., None]), 0.0)
        factor = jnp.exp(run_max - new_max)
        run_sum = run_sum * factor + jnp.sum(weights, axis=-1)
        scaled = (weights * value_scale.T[:, None, None, :]).astype(jnp.bfloat16)
        accumulate = accumulate * factor[..., None] + jnp.einsum(
            "kgrn,nkd->kgrd", scaled, value_tile, preferred_element_type=jnp.float32
        )
        return (new_max, run_sum, accumulate)

    def keep_state(current):
        return current

    return lax.cond(jnp.any(allowed), update, keep_state, totals)


def fold_packet(totals, packet, query_tile, query_pos, query_doc, starts, heads_kv):
    block_count = packet.shape[0]
    sub_blocks = math.gcd(block_count, max(1, 256 // BLK))
    step_count = block_count // sub_blocks
    key_count = sub_blocks * BLK
    key_part = packet[:, 0, :BLK, :].reshape(step_count, key_count, heads_kv, HD)
    value_part = packet[:, 1, :BLK, :].reshape(step_count, key_count, heads_kv, HD)
    key_scale = packet[:, 0, BLK, :].reshape(block_count, heads_kv, HD)[:, :, 0].astype(jnp.float32)
    value_scale = (
        packet[:, 1, BLK, :].reshape(block_count, heads_kv, HD)[:, :, 0].astype(jnp.float32)
    )
    key_scale = jnp.repeat(key_scale, BLK, axis=0).reshape(step_count, key_count, heads_kv)
    value_scale = jnp.repeat(value_scale, BLK, axis=0).reshape(step_count, key_count, heads_kv)
    offsets = jnp.arange(step_count, dtype=jnp.int32) * key_count

    def one_step(current, scan_item):
        key_tile, value_tile, key_sc, value_sc, offset = scan_item
        key_pos = offset + jnp.arange(key_count, dtype=jnp.int32)
        return (
            block_update(
                current,
                query_tile,
                query_pos,
                query_doc,
                key_tile,
                value_tile,
                key_sc,
                value_sc,
                key_pos,
                starts,
            ),
            None,
        )

    totals, _ = lax.scan(one_step, totals, (key_part, value_part, key_scale, value_scale, offsets))
    return totals


def finish(totals, value_means, heads_kv, group_size, row_count):
    run_max, run_sum, accumulate = totals
    result = accumulate / run_sum[..., None] + value_means.reshape(heads_kv, 1, 1, HD)
    return (
        result.transpose(2, 0, 1, 3)
        .reshape(row_count, heads_kv * group_size * HD)
        .astype(jnp.bfloat16)
    )


def shift_from(x, offset, count):
    pairs = [(i, (i + offset) % count) for i in range(count)]
    return lax.ppermute(x, "seq", pairs)


def gather_window(packet, count, depth):
    held = packet[None]
    for width, shifts in ((1, (1, 2, 3)), (4, (4, 8, 12)), (16, (16, 32))):
        parts = [held]
        for offset in shifts:
            need = min(width, depth - offset)
            if need > 0:
                parts.append(shift_from(held[:need], offset, count))
        held = jnp.concatenate(parts, axis=0)
    return held


def shards(queries, key_tokens, value_tokens, key_scales, value_scales, value_means, doc_lengths):
    local_keys, local_values = (
        lax.all_to_all(key_tokens, "head", split_axis=1, concat_axis=0, tiled=True),
        lax.all_to_all(value_tokens, "head", split_axis=1, concat_axis=0, tiled=True),
    )
    row_count = local_keys.shape[0]
    heads_kv = local_keys.shape[1] // HD
    group_size = QH // KVH
    blocks = row_count // BLK
    seq_count = lax.axis_size("seq")
    seq_index = lax.axis_index("seq")
    starts = jnp.cumsum(doc_lengths) - doc_lengths
    depth = min(seq_count, -(-(MOST - 1) // row_count) + 1)
    pad_rows = 8
    scale_rows = jnp.zeros((2, pad_rows, heads_kv * HD), jnp.bfloat16)
    scale_rows = scale_rows.at[0, :blocks].set(jnp.repeat(key_scales, HD, axis=1))
    scale_rows = scale_rows.at[1, :blocks].set(jnp.repeat(value_scales, HD, axis=1))
    packet = jnp.concatenate([jnp.stack([local_keys, local_values]), scale_rows], axis=1)
    window = gather_window(packet, seq_count, depth)
    slots = window.shape[0]
    pair = 2
    padded = -(-slots // pair) * pair
    window = jnp.concatenate(
        [window, jnp.zeros((padded - slots,) + window.shape[1:], window.dtype)], axis=0
    )
    shard_of = (seq_index - jnp.arange(padded, dtype=jnp.int32)) % seq_count
    key_pos = shard_of[:, None] * row_count + jnp.arange(row_count, dtype=jnp.int32)[None, :]
    key_pos = jnp.where(jnp.arange(padded)[:, None] < slots, key_pos, jnp.int32(2**30))
    steps = padded // pair
    key_count = pair * row_count
    key_part = window[:, 0, :row_count].reshape(steps, key_count, heads_kv, HD)
    value_part = window[:, 1, :row_count].reshape(steps, key_count, heads_kv, HD)
    key_sc = jnp.repeat(window[:, 0, row_count:row_count + blocks, ::HD], BLK, axis=1)
    value_sc = jnp.repeat(window[:, 1, row_count:row_count + blocks, ::HD], BLK, axis=1)
    key_sc = key_sc.astype(jnp.float32).reshape(steps, key_count, heads_kv)
    value_sc = value_sc.astype(jnp.float32).reshape(steps, key_count, heads_kv)
    key_pos = key_pos.reshape(steps, key_count)

    own_pos = seq_index * row_count + jnp.arange(row_count, dtype=jnp.int32)
    query_tile = queries.reshape(row_count, heads_kv, group_size, HD).transpose(1, 2, 0, 3)
    query_doc = doc_index(own_pos, starts)
    initial = (
        jnp.full((heads_kv, group_size, row_count), NEG, jnp.float32),
        jnp.zeros((heads_kv, group_size, row_count), jnp.float32),
        jnp.zeros((heads_kv, group_size, row_count, HD), jnp.float32),
    )

    def one_step(current, scan_item):
        k_tile, v_tile, k_sc, v_sc, pos = scan_item
        return (
            block_update(
                current, query_tile, own_pos, query_doc, k_tile, v_tile, k_sc, v_sc, pos, starts
            ),
            None,
        )

    totals, _ = lax.scan(one_step, initial, (key_part, value_part, key_sc, value_sc, key_pos))
    return finish(totals, value_means, heads_kv, group_size, row_count)


def solution(mesh):
    in_specs = (
        P("seq", "head"),
        P(("seq", "head"), None),
        P(("seq", "head"), None),
        P("seq", "head"),
        P("seq", "head"),
        P("head"),
        P(),
    )
    out_specs = P("seq", "head")
    return jax.shard_map(shards, mesh=mesh, in_specs=in_specs, out_specs=out_specs, check_vma=False)
```

```python
import math

import jax
import jax.numpy as jnp
from jax import lax
from jax.experimental import pallas as pl
from jax.experimental.pallas import tpu as pltpu
from jax.sharding import PartitionSpec as P

QH = 64
KVH = 8
HD = 128
BLK = 64
MOST = 5120


NEG = -1e30


def doc_index(positions, starts):
    return jnp.sum((starts[None, :] <= positions[:, None]).astype(jnp.int32), axis=1) - 1


def block_update(
    totals,
    query_tile,
    query_pos,
    query_doc,
    key_tile,
    value_tile,
    key_scale,
    value_scale,
    key_pos,
    starts,
):
    inv_scale = 1.0 / math.sqrt(HD)
    key_doc = doc_index(key_pos, starts)
    allowed = (key_doc[None, :] == query_doc[:, None]) & (key_pos[None, :] <= query_pos[:, None])

    def update(current):
        run_max, run_sum, accumulate = current
        scores = jnp.einsum(
            "kgrd,nkd->kgrn", query_tile, key_tile, preferred_element_type=jnp.float32
        )
        scores = scores * (key_scale.T * inv_scale)[:, None, None, :]
        scores = jnp.where(allowed[None, None], scores, NEG)
        new_max = jnp.maximum(run_max, jnp.max(scores, axis=-1))
        weights = jnp.where(allowed[None, None], jnp.exp(scores - new_max[..., None]), 0.0)
        factor = jnp.exp(run_max - new_max)
        run_sum = run_sum * factor + jnp.sum(weights, axis=-1)
        scaled = (weights * value_scale.T[:, None, None, :]).astype(jnp.bfloat16)
        accumulate = accumulate * factor[..., None] + jnp.einsum(
            "kgrn,nkd->kgrd", scaled, value_tile, preferred_element_type=jnp.float32
        )
        return (new_max, run_sum, accumulate)

    def keep_state(current):
        return current

    return lax.cond(jnp.any(allowed), update, keep_state, totals)


def fold_packet(totals, packet, query_tile, query_pos, query_doc, starts, heads_kv):
    block_count = packet.shape[0]
    sub_blocks = math.gcd(block_count, max(1, 256 // BLK))
    step_count = block_count // sub_blocks
    key_count = sub_blocks * BLK
    key_part = packet[:, 0, :BLK, :].reshape(step_count, key_count, heads_kv, HD)
    value_part = packet[:, 1, :BLK, :].reshape(step_count, key_count, heads_kv, HD)
    key_scale = packet[:, 0, BLK, :].reshape(block_count, heads_kv, HD)[:, :, 0].astype(jnp.float32)
    value_scale = (
        packet[:, 1, BLK, :].reshape(block_count, heads_kv, HD)[:, :, 0].astype(jnp.float32)
    )
    key_scale = jnp.repeat(key_scale, BLK, axis=0).reshape(step_count, key_count, heads_kv)
    value_scale = jnp.repeat(value_scale, BLK, axis=0).reshape(step_count, key_count, heads_kv)
    offsets = jnp.arange(step_count, dtype=jnp.int32) * key_count

    def one_step(current, scan_item):
        key_tile, value_tile, key_sc, value_sc, offset = scan_item
        key_pos = offset + jnp.arange(key_count, dtype=jnp.int32)
        return (
            block_update(
                current,
                query_tile,
                query_pos,
                query_doc,
                key_tile,
                value_tile,
                key_sc,
                value_sc,
                key_pos,
                starts,
            ),
            None,
        )

    totals, _ = lax.scan(one_step, totals, (key_part, value_part, key_scale, value_scale, offsets))
    return totals


def finish(totals, value_means, heads_kv, group_size, row_count):
    run_max, run_sum, accumulate = totals
    result = accumulate / run_sum[..., None] + value_means.reshape(heads_kv, 1, 1, HD)
    return (
        result.transpose(2, 0, 1, 3)
        .reshape(row_count, heads_kv * group_size * HD)
        .astype(jnp.bfloat16)
    )


def shift_from(x, offset, count):
    pairs = [(i, (i + offset) % count) for i in range(count)]
    return lax.ppermute(x, "seq", pairs)


def gather_window(packet, count, depth):
    held = packet[None]
    for width, shifts in ((1, (1, 2, 3)), (4, (4, 8, 12)), (16, (16, 32))):
        parts = [held]
        for offset in shifts:
            need = min(width, depth - offset)
            if need > 0:
                parts.append(shift_from(held[:need], offset, count))
        held = jnp.concatenate(parts, axis=0)
    return held


def attention_kernel(
    info_ref, query_ref, window_ref, low_ref, mean_ref, out_ref, max_ref, sum_ref, acc_ref
):
    rows = query_ref.shape[0]
    group_size = query_ref.shape[1] // HD
    inv_scale = 1.0 / math.sqrt(HD)
    seq_index = info_ref[0]
    used = info_ref[1]
    max_ref[...] = jnp.full(max_ref.shape, NEG, jnp.float32)
    sum_ref[...] = jnp.zeros(sum_ref.shape, jnp.float32)
    acc_ref[...] = jnp.zeros(acc_ref.shape, jnp.float32)
    query_pos = seq_index * rows + lax.broadcasted_iota(jnp.int32, (rows, rows), 0)
    low = low_ref[...]
    lane = lax.broadcasted_iota(jnp.int32, (rows, rows), 1)
    lane_row = lax.broadcasted_iota(jnp.int32, (1, rows), 1)

    def one_slot(slot, carry):
        key_pos = (seq_index - slot) * rows + lane
        allowed = (key_pos <= query_pos) & (key_pos >= low)
        key_tile = window_ref[slot, 0, :rows, :]
        value_tile = window_ref[slot, 1, :rows, :]
        key_rows = window_ref[slot, 0, rows:rows + 8, :].astype(jnp.float32)
        value_rows = window_ref[slot, 1, rows:rows + 8, :].astype(jnp.float32)
        key_scale = jnp.where(lane_row < BLK, key_rows[0:1], key_rows[1:2]) * inv_scale
        value_scale = jnp.where(lane_row < BLK, value_rows[0:1], value_rows[1:2])
        for g in range(group_size):
            query_tile = query_ref[:, g * HD:(g + 1) * HD]
            scores = lax.dot_general(
                query_tile, key_tile, (((1,), (1,)), ((), ())), preferred_element_type=jnp.float32
            )
            scores = jnp.where(allowed, scores * key_scale, NEG)
            run_max = max_ref[g][:, :1]
            new_max = jnp.maximum(run_max, jnp.max(scores, axis=1, keepdims=True))
            weights = jnp.where(allowed, jnp.exp(scores - new_max), 0.0)
            factor = jnp.exp(run_max - new_max)
            run_sum = sum_ref[g][:, :1] * factor + jnp.sum(weights, axis=1, keepdims=True)
            scaled = (weights * value_scale).astype(jnp.bfloat16)
            acc_ref[g] = acc_ref[g] * factor + jnp.dot(
                scaled, value_tile, preferred_element_type=jnp.float32
            )
            max_ref[g] = jnp.broadcast_to(new_max, (rows, HD))
            sum_ref[g] = jnp.broadcast_to(run_sum, (rows, HD))
        return carry

    lax.fori_loop(0, used, one_slot, 0)
    mean = mean_ref[...]
    for g in range(group_size):
        out_ref[:, g * HD:(g + 1) * HD] = (acc_ref[g] / sum_ref[g] + mean).astype(jnp.bfloat16)


def attend(info, queries, window, low, mean):
    rows, width = queries.shape
    group_size = width // HD
    full = lambda shape: pl.BlockSpec(shape, lambda i, info: (0,) * len(shape))
    return pl.pallas_call(
        attention_kernel,
        out_shape=jax.ShapeDtypeStruct((rows, width), jnp.bfloat16),
        grid_spec=pltpu.PrefetchScalarGridSpec(
            num_scalar_prefetch=1,
            grid=(1,),
            in_specs=[full(queries.shape), full(window.shape), full(low.shape), full(mean.shape)],
            out_specs=full((rows, width)),
            scratch_shapes=[pltpu.VMEM((group_size, rows, HD), jnp.float32)] * 3,
        ),
    )(info, queries, window, low, mean)


def shards(queries, key_tokens, value_tokens, key_scales, value_scales, value_means, doc_lengths):
    local_keys, local_values = (
        lax.all_to_all(key_tokens, "head", split_axis=1, concat_axis=0, tiled=True),
        lax.all_to_all(value_tokens, "head", split_axis=1, concat_axis=0, tiled=True),
    )
    row_count = local_keys.shape[0]
    heads_kv = local_keys.shape[1] // HD
    group_size = QH // KVH
    blocks = row_count // BLK
    seq_count = lax.axis_size("seq")
    seq_index = lax.axis_index("seq")
    starts = jnp.cumsum(doc_lengths) - doc_lengths
    depth = min(seq_count, -(-(MOST - 1) // row_count) + 1)
    pad_rows = 8
    scale_rows = jnp.zeros((2, pad_rows, heads_kv * HD), jnp.bfloat16)
    scale_rows = scale_rows.at[0, :blocks].set(jnp.repeat(key_scales, HD, axis=1))
    scale_rows = scale_rows.at[1, :blocks].set(jnp.repeat(value_scales, HD, axis=1))
    packet = jnp.concatenate([jnp.stack([local_keys, local_values]), scale_rows], axis=1)
    window = gather_window(packet, seq_count, depth)
    slots = window.shape[0]
    own_pos = seq_index * row_count + jnp.arange(row_count, dtype=jnp.int32)
    low = starts[doc_index(own_pos, starts)]
    used = jnp.clip(seq_index - low[0] // row_count + 1, 1, slots).astype(jnp.int32)
    info = jnp.stack([seq_index.astype(jnp.int32), used])
    low_tile = jnp.broadcast_to(low[:, None], (row_count, row_count)).astype(jnp.int32)
    mean = value_means.reshape(1, HD)
    return attend(info, queries, window, low_tile, mean)


def solution(mesh):
    in_specs = (
        P("seq", "head"),
        P(("seq", "head"), None),
        P(("seq", "head"), None),
        P("seq", "head"),
        P("seq", "head"),
        P("head"),
        P(),
    )
    out_specs = P("seq", "head")
    return jax.shard_map(shards, mesh=mesh, in_specs=in_specs, out_specs=out_specs, check_vma=False)
```

```python
import math

import jax
import jax.numpy as jnp
from jax import lax
from jax.experimental import pallas as pl
from jax.experimental.pallas import tpu as pltpu
from jax.sharding import PartitionSpec as P

QH = 64
KVH = 8
HD = 128
BLK = 64
MOST = 5120


NEG = -1e30


def doc_index(positions, starts):
    return jnp.sum((starts[None, :] <= positions[:, None]).astype(jnp.int32), axis=1) - 1


def block_update(
    totals,
    query_tile,
    query_pos,
    query_doc,
    key_tile,
    value_tile,
    key_scale,
    value_scale,
    key_pos,
    starts,
):
    inv_scale = 1.0 / math.sqrt(HD)
    key_doc = doc_index(key_pos, starts)
    allowed = (key_doc[None, :] == query_doc[:, None]) & (key_pos[None, :] <= query_pos[:, None])

    def update(current):
        run_max, run_sum, accumulate = current
        scores = jnp.einsum(
            "kgrd,nkd->kgrn", query_tile, key_tile, preferred_element_type=jnp.float32
        )
        scores = scores * (key_scale.T * inv_scale)[:, None, None, :]
        scores = jnp.where(allowed[None, None], scores, NEG)
        new_max = jnp.maximum(run_max, jnp.max(scores, axis=-1))
        weights = jnp.where(allowed[None, None], jnp.exp(scores - new_max[..., None]), 0.0)
        factor = jnp.exp(run_max - new_max)
        run_sum = run_sum * factor + jnp.sum(weights, axis=-1)
        scaled = (weights * value_scale.T[:, None, None, :]).astype(jnp.bfloat16)
        accumulate = accumulate * factor[..., None] + jnp.einsum(
            "kgrn,nkd->kgrd", scaled, value_tile, preferred_element_type=jnp.float32
        )
        return (new_max, run_sum, accumulate)

    def keep_state(current):
        return current

    return lax.cond(jnp.any(allowed), update, keep_state, totals)


def fold_packet(totals, packet, query_tile, query_pos, query_doc, starts, heads_kv):
    block_count = packet.shape[0]
    sub_blocks = math.gcd(block_count, max(1, 256 // BLK))
    step_count = block_count // sub_blocks
    key_count = sub_blocks * BLK
    key_part = packet[:, 0, :BLK, :].reshape(step_count, key_count, heads_kv, HD)
    value_part = packet[:, 1, :BLK, :].reshape(step_count, key_count, heads_kv, HD)
    key_scale = packet[:, 0, BLK, :].reshape(block_count, heads_kv, HD)[:, :, 0].astype(jnp.float32)
    value_scale = (
        packet[:, 1, BLK, :].reshape(block_count, heads_kv, HD)[:, :, 0].astype(jnp.float32)
    )
    key_scale = jnp.repeat(key_scale, BLK, axis=0).reshape(step_count, key_count, heads_kv)
    value_scale = jnp.repeat(value_scale, BLK, axis=0).reshape(step_count, key_count, heads_kv)
    offsets = jnp.arange(step_count, dtype=jnp.int32) * key_count

    def one_step(current, scan_item):
        key_tile, value_tile, key_sc, value_sc, offset = scan_item
        key_pos = offset + jnp.arange(key_count, dtype=jnp.int32)
        return (
            block_update(
                current,
                query_tile,
                query_pos,
                query_doc,
                key_tile,
                value_tile,
                key_sc,
                value_sc,
                key_pos,
                starts,
            ),
            None,
        )

    totals, _ = lax.scan(one_step, totals, (key_part, value_part, key_scale, value_scale, offsets))
    return totals


def finish(totals, value_means, heads_kv, group_size, row_count):
    run_max, run_sum, accumulate = totals
    result = accumulate / run_sum[..., None] + value_means.reshape(heads_kv, 1, 1, HD)
    return (
        result.transpose(2, 0, 1, 3)
        .reshape(row_count, heads_kv * group_size * HD)
        .astype(jnp.bfloat16)
    )


def shift_from(x, offset, count):
    pairs = [(i, (i + offset) % count) for i in range(count)]
    return lax.ppermute(x, "seq", pairs)


def gather_window(packet, count, depth):
    held = packet[None]
    for width, shifts in ((1, (1, 2, 3)), (4, (4, 8, 12)), (16, (16, 32))):
        parts = [held]
        for offset in shifts:
            need = min(width, depth - offset)
            if need > 0:
                parts.append(shift_from(held[:need], offset, count))
        held = jnp.concatenate(parts, axis=0)
    return held


def attention_kernel(
    info_ref, query_ref, window_ref, low_ref, mean_ref, out_ref, max_ref, sum_ref, acc_ref
):
    group_size, rows, _ = acc_ref.shape
    inv_scale = 1.0 / math.sqrt(HD)
    seq_index = info_ref[0]
    pairs = info_ref[1]
    max_ref[...] = jnp.full(max_ref.shape, NEG, jnp.float32)
    sum_ref[...] = jnp.zeros(sum_ref.shape, jnp.float32)
    acc_ref[...] = jnp.zeros(acc_ref.shape, jnp.float32)
    query_pos = seq_index * rows + lax.broadcasted_iota(jnp.int32, (rows, rows), 0)
    low = low_ref[...]
    lane = lax.broadcasted_iota(jnp.int32, (rows, rows), 1)
    query_all = query_ref[...]

    def one_pair(pair, carry):
        parts = []
        for half in range(2):
            slot = 2 * pair + half
            key_pos = (seq_index - slot) * rows + lane
            allowed = ((key_pos <= query_pos) & (key_pos >= low))[None]
            key_t = window_ref[slot, 0, :HD, :]
            key_scale = window_ref[slot, 0, HD:HD + 1, :].astype(jnp.float32) * inv_scale
            value_scale = window_ref[slot, 1, rows:rows + 1, :].astype(jnp.float32)
            scores = jnp.dot(query_all, key_t, preferred_element_type=jnp.float32)
            scores = scores.reshape(group_size, rows, rows) * key_scale[None]
            scores = jnp.where(allowed, scores, NEG)
            parts.append((scores, allowed, value_scale[None], slot))
        run_max = max_ref[...][:, :, :1]
        new_max = run_max
        for scores, _, _, _ in parts:
            new_max = jnp.maximum(new_max, jnp.max(scores, axis=2, keepdims=True))
        factor = jnp.exp(run_max - new_max)
        run_sum = sum_ref[...][:, :, :1] * factor
        acc = acc_ref[...] * factor
        for scores, allowed, value_scale, slot in parts:
            weights = jnp.where(allowed, jnp.exp(scores - new_max), 0.0)
            run_sum = run_sum + jnp.sum(weights, axis=2, keepdims=True)
            scaled = (weights * value_scale).astype(jnp.bfloat16).reshape(group_size * rows, rows)
            value_tile = window_ref[slot, 1, :rows, :]
            mixed = jnp.dot(scaled, value_tile, preferred_element_type=jnp.float32)
            acc = acc + mixed.reshape(group_size, rows, HD)
        acc_ref[...] = acc
        max_ref[...] = jnp.broadcast_to(new_max, max_ref.shape)
        sum_ref[...] = jnp.broadcast_to(run_sum, sum_ref.shape)
        return carry

    lax.fori_loop(0, pairs, one_pair, 0)
    result = acc_ref[...] / sum_ref[...] + mean_ref[...][None]
    for g in range(group_size):
        out_ref[:, g * HD:(g + 1) * HD] = result[g].astype(jnp.bfloat16)


def attend(info, queries, window, low, mean):
    rows, width = queries.shape
    group_size = width // HD
    query_all = queries.reshape(rows, group_size, HD).transpose(1, 0, 2).reshape(-1, HD)
    full = lambda shape: pl.BlockSpec(shape, lambda i, info: (0,) * len(shape))
    return pl.pallas_call(
        attention_kernel,
        out_shape=jax.ShapeDtypeStruct((rows, width), jnp.bfloat16),
        grid_spec=pltpu.PrefetchScalarGridSpec(
            num_scalar_prefetch=1,
            grid=(1,),
            in_specs=[full(query_all.shape), full(window.shape), full(low.shape), full(mean.shape)],
            out_specs=full((rows, width)),
            scratch_shapes=[pltpu.VMEM((group_size, rows, HD), jnp.float32)] * 3,
        ),
    )(info, query_all, window, low, mean)


def shards(queries, key_tokens, value_tokens, key_scales, value_scales, value_means, doc_lengths):
    local_keys, local_values = (
        lax.all_to_all(key_tokens, "head", split_axis=1, concat_axis=0, tiled=True),
        lax.all_to_all(value_tokens, "head", split_axis=1, concat_axis=0, tiled=True),
    )
    row_count = local_keys.shape[0]
    heads_kv = local_keys.shape[1] // HD
    group_size = QH // KVH
    blocks = row_count // BLK
    seq_count = lax.axis_size("seq")
    seq_index = lax.axis_index("seq")
    starts = jnp.cumsum(doc_lengths) - doc_lengths
    depth = min(seq_count, -(-(MOST - 1) // row_count) + 1)
    pad_rows = 8
    key_scale_row = jnp.repeat(key_scales.reshape(-1), BLK)
    value_scale_row = jnp.repeat(value_scales.reshape(-1), BLK)
    scale_rows = jnp.zeros((2, pad_rows, row_count), jnp.bfloat16)
    scale_rows = scale_rows.at[0, 0].set(key_scale_row).at[1, 0].set(value_scale_row)
    packet = jnp.concatenate([jnp.stack([local_keys.T, local_values]), scale_rows], axis=1)
    window = gather_window(packet, seq_count, depth)
    slots = window.shape[0]
    window = jnp.concatenate(
        [window, jnp.zeros((slots % 2,) + window.shape[1:], window.dtype)], axis=0
    )
    own_pos = seq_index * row_count + jnp.arange(row_count, dtype=jnp.int32)
    low = starts[doc_index(own_pos, starts)]
    used = jnp.clip(seq_index - low[0] // row_count + 1, 1, slots).astype(jnp.int32)
    info = jnp.stack([seq_index.astype(jnp.int32), (used + 1) // 2])
    low_tile = jnp.broadcast_to(low[:, None], (row_count, row_count)).astype(jnp.int32)
    mean = value_means.reshape(1, HD)
    return attend(info, queries, window, low_tile, mean)


def solution(mesh):
    in_specs = (
        P("seq", "head"),
        P(("seq", "head"), None),
        P(("seq", "head"), None),
        P("seq", "head"),
        P("seq", "head"),
        P("head"),
        P(),
    )
    out_specs = P("seq", "head")
    return jax.shard_map(shards, mesh=mesh, in_specs=in_specs, out_specs=out_specs, check_vma=False)
```

```python
import functools
import math

import jax
import jax.numpy as jnp
from jax import lax
from jax.experimental import pallas as pl
from jax.experimental.pallas import tpu as pltpu
from jax.sharding import PartitionSpec as P

QH = 64
KVH = 8
HD = 128
BLK = 64
MOST = 5120

NEG = -1e30


def doc_index(positions, starts):
    return jnp.sum((starts[None, :] <= positions[:, None]).astype(jnp.int32), axis=1) - 1


def shift_from(x, offset, count):
    pairs = [(i, (i + offset) % count) for i in range(count)]
    return lax.ppermute(x, "seq", pairs)


def gather_stages(packet, count, depth):
    held = packet[None]
    stages = [held]
    for width, shifts in ((1, (1, 2, 3)), (4, (4, 8, 12)), (16, (16, 32))):
        parts = []
        for offset in shifts:
            need = min(width, depth - offset)
            if need > 0:
                parts.append(shift_from(held[:need], offset, count))
        stages.append(parts)
        held = jnp.concatenate([held] + parts, axis=0)
    return stages


def attention_kernel(first, last, offset, *refs):
    info_ref, query_ref, window_ref, low_ref, mean_ref = refs[:5]
    rest = refs[5:]
    if not first:
        max_in, sum_in, acc_in = rest[:3]
        rest = rest[3:]
    if last:
        out_ref = rest[0]
        rest = rest[1:]
    else:
        max_out, sum_out, acc_out = rest[:3]
        rest = rest[3:]
    max_ref, sum_ref, acc_ref = rest
    group_size, rows, _ = acc_ref.shape
    inv_scale = 1.0 / math.sqrt(HD)
    seq_index = info_ref[0]
    pairs = info_ref[1]
    if first:
        max_ref[...] = jnp.full(max_ref.shape, NEG, jnp.float32)
        sum_ref[...] = jnp.zeros(sum_ref.shape, jnp.float32)
        acc_ref[...] = jnp.zeros(acc_ref.shape, jnp.float32)
    else:
        max_ref[...] = max_in[...]
        sum_ref[...] = sum_in[...]
        acc_ref[...] = acc_in[...]
    query_pos = seq_index * rows + lax.broadcasted_iota(jnp.int32, (rows, rows), 0)
    low = low_ref[...]
    lane = lax.broadcasted_iota(jnp.int32, (rows, rows), 1)
    query_all = query_ref[...]

    def one_pair(pair, carry):
        parts = []
        for half in range(2):
            slot = 2 * pair + half
            key_pos = (seq_index - offset - slot) * rows + lane
            allowed = ((key_pos <= query_pos) & (key_pos >= low))[None]
            key_t = window_ref[slot, 0, :HD, :]
            key_scale = window_ref[slot, 0, HD:HD + 1, :].astype(jnp.float32) * inv_scale
            value_scale = window_ref[slot, 1, rows:rows + 1, :].astype(jnp.float32)
            scores = jnp.dot(query_all, key_t, preferred_element_type=jnp.float32)
            scores = scores.reshape(group_size, rows, rows) * key_scale[None]
            scores = jnp.where(allowed, scores, NEG)
            parts.append((scores, allowed, value_scale[None], slot))
        run_max = max_ref[...][:, :, :1]
        new_max = run_max
        for scores, _, _, _ in parts:
            new_max = jnp.maximum(new_max, jnp.max(scores, axis=2, keepdims=True))
        factor = jnp.exp(run_max - new_max)
        run_sum = sum_ref[...][:, :, :1] * factor
        acc = acc_ref[...] * factor
        for scores, allowed, value_scale, slot in parts:
            weights = jnp.where(allowed, jnp.exp(scores - new_max), 0.0)
            run_sum = run_sum + jnp.sum(weights, axis=2, keepdims=True)
            scaled = (weights * value_scale).astype(jnp.bfloat16).reshape(group_size * rows, rows)
            value_tile = window_ref[slot, 1, :rows, :]
            mixed = jnp.dot(scaled, value_tile, preferred_element_type=jnp.float32)
            acc = acc + mixed.reshape(group_size, rows, HD)
        acc_ref[...] = acc
        max_ref[...] = jnp.broadcast_to(new_max, max_ref.shape)
        sum_ref[...] = jnp.broadcast_to(run_sum, sum_ref.shape)
        return carry

    lax.fori_loop(0, pairs, one_pair, 0)
    if last:
        result = acc_ref[...] / sum_ref[...] + mean_ref[...][None]
        for g in range(group_size):
            out_ref[:, g * HD:(g + 1) * HD] = result[g].astype(jnp.bfloat16)
    else:
        max_out[...] = max_ref[...]
        sum_out[...] = sum_ref[...]
        acc_out[...] = acc_ref[...]


def attend_part(info, query_all, window, low, mean, state, offset, last, width):
    group_size = query_all.shape[0] // HD
    rows = low.shape[0]
    full = lambda shape: pl.BlockSpec(shape, lambda i, info: (0,) * len(shape))
    state_shape = jax.ShapeDtypeStruct((group_size, rows, HD), jnp.float32)
    operands = [query_all, window, low, mean] + ([] if state is None else list(state))
    if last:
        out_shape = jax.ShapeDtypeStruct((rows, width), jnp.bfloat16)
        out_specs = full((rows, width))
    else:
        out_shape = (state_shape,) * 3
        out_specs = (full(state_shape.shape),) * 3
    kernel = functools.partial(attention_kernel, state is None, last, offset)
    return pl.pallas_call(
        kernel,
        out_shape=out_shape,
        grid_spec=pltpu.PrefetchScalarGridSpec(
            num_scalar_prefetch=1,
            grid=(1,),
            in_specs=[full(x.shape) for x in operands],
            out_specs=out_specs,
            scratch_shapes=[pltpu.VMEM((group_size, rows, HD), jnp.float32)] * 3,
        ),
    )(info, *operands)


def shards(queries, key_tokens, value_tokens, key_scales, value_scales, value_means, doc_lengths):
    heads = lax.axis_size("head")
    both = jnp.stack([key_tokens, value_tokens], axis=1)
    both = both.reshape(both.shape[0], 2, heads, -1)
    both = lax.all_to_all(both, "head", split_axis=2, concat_axis=0, tiled=True)
    local_keys = both[:, 0, 0]
    local_values = both[:, 1, 0]
    row_count = local_keys.shape[0]
    group_size = QH // KVH
    seq_count = lax.axis_size("seq")
    seq_index = lax.axis_index("seq")
    starts = jnp.cumsum(doc_lengths) - doc_lengths
    depth = min(seq_count, -(-(MOST - 1) // row_count) + 1)
    pad_rows = 8
    key_scale_row = jnp.repeat(key_scales.reshape(-1), BLK)
    value_scale_row = jnp.repeat(value_scales.reshape(-1), BLK)
    scale_rows = jnp.zeros((2, pad_rows, row_count), jnp.bfloat16)
    scale_rows = scale_rows.at[0, 0].set(key_scale_row).at[1, 0].set(value_scale_row)
    packet = jnp.concatenate([jnp.stack([local_keys.T, local_values]), scale_rows], axis=1)
    stages = gather_stages(packet, seq_count, depth)
    own_pos = seq_index * row_count + jnp.arange(row_count, dtype=jnp.int32)
    low = starts[doc_index(own_pos, starts)]
    used = jnp.clip(seq_index - low[0] // row_count + 1, 1, depth).astype(jnp.int32)
    low_tile = jnp.broadcast_to(low[:, None], (row_count, row_count)).astype(jnp.int32)
    mean = value_means.reshape(1, HD)
    query_all = queries.reshape(row_count, group_size, HD).transpose(1, 0, 2).reshape(-1, HD)
    chunks = [
        jnp.concatenate([stages[0]] + stages[1], axis=0),
        jnp.concatenate(stages[2], axis=0),
        jnp.concatenate(stages[3], axis=0),
    ]
    state = None
    offset = 0
    for index, chunk in enumerate(chunks):
        slots = chunk.shape[0]
        if slots % 2:
            chunk = jnp.concatenate([chunk, jnp.zeros((1,) + chunk.shape[1:], chunk.dtype)])
        pairs = jnp.clip((used - offset + 1) // 2, 0, chunk.shape[0] // 2).astype(jnp.int32)
        info = jnp.stack([seq_index.astype(jnp.int32), pairs])
        last = index == len(chunks) - 1
        state = attend_part(
            info, query_all, chunk, low_tile, mean, state, offset, last, queries.shape[1]
        )
        offset += slots
    return state


def solution(mesh):
    in_specs = (
        P("seq", "head"),
        P(("seq", "head"), None),
        P(("seq", "head"), None),
        P("seq", "head"),
        P("seq", "head"),
        P("head"),
        P(),
    )
    out_specs = P("seq", "head")
    return jax.shard_map(shards, mesh=mesh, in_specs=in_specs, out_specs=out_specs, check_vma=False)
```

```python
import functools
import math

import jax
import jax.numpy as jnp
from jax import lax
from jax.experimental import pallas as pl
from jax.experimental.pallas import tpu as pltpu
from jax.sharding import PartitionSpec as P

QH = 64
KVH = 8
HD = 128
BLK = 64
MOST = 5120

NEG = -1e30


def doc_index(positions, starts):
    return jnp.sum((starts[None, :] <= positions[:, None]).astype(jnp.int32), axis=1) - 1


def shift_from(x, offset, count):
    pairs = [(i, (i + offset) % count) for i in range(count)]
    return lax.ppermute(x, "seq", pairs)


def gather_stages(packet, count, depth):
    held = packet[None]
    stages = [held]
    for width, shifts in ((1, (1, 2, 3)), (4, (4, 8, 12)), (16, (16, 32))):
        parts = []
        for offset in shifts:
            need = min(width, depth - offset)
            if need > 0:
                parts.append(shift_from(held[:need], offset, count))
        stages.append(parts)
        held = jnp.concatenate([held] + parts, axis=0)
    return stages


def attention_kernel(first, last, offset, *refs):
    info_ref, query_ref, window_ref, low_ref, mean_ref = refs[:5]
    rest = refs[5:]
    if not first:
        max_in, sum_in, acc_in = rest[:3]
        rest = rest[3:]
    if last:
        out_ref = rest[0]
        rest = rest[1:]
    else:
        max_out, sum_out, acc_out = rest[:3]
        rest = rest[3:]
    max_ref, sum_ref, acc_ref = rest
    group_size, rows, _ = acc_ref.shape
    inv_scale = 1.0 / math.sqrt(HD)
    seq_index = info_ref[0]
    pairs = info_ref[1]
    if first:
        max_ref[...] = jnp.full(max_ref.shape, NEG, jnp.float32)
        sum_ref[...] = jnp.zeros(sum_ref.shape, jnp.float32)
        acc_ref[...] = jnp.zeros(acc_ref.shape, jnp.float32)
    else:
        max_ref[...] = max_in[...]
        sum_ref[...] = sum_in[...]
        acc_ref[...] = acc_in[...]
    query_pos = seq_index * rows + lax.broadcasted_iota(jnp.int32, (rows, rows), 0)
    low = low_ref[...]
    lane = lax.broadcasted_iota(jnp.int32, (rows, rows), 1)
    query_all = query_ref[...]

    low_top = info_ref[2]

    def fold_pair(pair, masked):
        parts = []
        for half in range(2):
            slot = 2 * pair + half
            key_t = window_ref[slot, 0, :HD, :]
            key_scale = window_ref[slot, 0, HD:HD + 1, :].astype(jnp.float32) * inv_scale
            value_scale = window_ref[slot, 1, rows:rows + 1, :].astype(jnp.float32)
            scores = jnp.dot(query_all, key_t, preferred_element_type=jnp.float32)
            scores = scores.reshape(group_size, rows, rows) * key_scale[None]
            allowed = None
            if masked:
                key_pos = (seq_index - offset - slot) * rows + lane
                allowed = ((key_pos <= query_pos) & (key_pos >= low))[None]
                scores = jnp.where(allowed, scores, NEG)
            parts.append((scores, allowed, value_scale[None], slot))
        run_max = max_ref[...][:, :, :1]
        new_max = run_max
        for scores, _, _, _ in parts:
            new_max = jnp.maximum(new_max, jnp.max(scores, axis=2, keepdims=True))
        factor = jnp.exp(run_max - new_max)
        run_sum = sum_ref[...][:, :, :1] * factor
        acc = acc_ref[...] * factor
        for scores, allowed, value_scale, slot in parts:
            weights = jnp.exp(scores - new_max)
            if masked:
                weights = jnp.where(allowed, weights, 0.0)
            run_sum = run_sum + jnp.sum(weights, axis=2, keepdims=True)
            scaled = (weights * value_scale).astype(jnp.bfloat16).reshape(group_size * rows, rows)
            value_tile = window_ref[slot, 1, :rows, :]
            mixed = jnp.dot(scaled, value_tile, preferred_element_type=jnp.float32)
            acc = acc + mixed.reshape(group_size, rows, HD)
        acc_ref[...] = acc
        max_ref[...] = jnp.broadcast_to(new_max, max_ref.shape)
        sum_ref[...] = jnp.broadcast_to(run_sum, sum_ref.shape)

    def one_pair(pair, carry):
        nearest = offset + 2 * pair
        inside = (nearest >= 1) & ((seq_index - nearest - 1) * rows >= low_top)
        lax.cond(inside, lambda: fold_pair(pair, False), lambda: fold_pair(pair, True))
        return carry

    lax.fori_loop(0, pairs, one_pair, 0)
    if last:
        result = acc_ref[...] / sum_ref[...] + mean_ref[...][None]
        for g in range(group_size):
            out_ref[:, g * HD:(g + 1) * HD] = result[g].astype(jnp.bfloat16)
    else:
        max_out[...] = max_ref[...]
        sum_out[...] = sum_ref[...]
        acc_out[...] = acc_ref[...]


def attend_part(info, query_all, window, low, mean, state, offset, last, width):
    group_size = query_all.shape[0] // HD
    rows = low.shape[0]
    full = lambda shape: pl.BlockSpec(shape, lambda i, info: (0,) * len(shape))
    state_shape = jax.ShapeDtypeStruct((group_size, rows, HD), jnp.float32)
    operands = [query_all, window, low, mean] + ([] if state is None else list(state))
    if last:
        out_shape = jax.ShapeDtypeStruct((rows, width), jnp.bfloat16)
        out_specs = full((rows, width))
    else:
        out_shape = (state_shape,) * 3
        out_specs = (full(state_shape.shape),) * 3
    kernel = functools.partial(attention_kernel, state is None, last, offset)
    return pl.pallas_call(
        kernel,
        out_shape=out_shape,
        grid_spec=pltpu.PrefetchScalarGridSpec(
            num_scalar_prefetch=1,
            grid=(1,),
            in_specs=[full(x.shape) for x in operands],
            out_specs=out_specs,
            scratch_shapes=[pltpu.VMEM((group_size, rows, HD), jnp.float32)] * 3,
        ),
    )(info, *operands)


def shards(queries, key_tokens, value_tokens, key_scales, value_scales, value_means, doc_lengths):
    heads = lax.axis_size("head")
    both = jnp.stack([key_tokens, value_tokens], axis=1)
    both = both.reshape(both.shape[0], 2, heads, -1)
    both = lax.all_to_all(both, "head", split_axis=2, concat_axis=0, tiled=True)
    local_keys = both[:, 0, 0]
    local_values = both[:, 1, 0]
    row_count = local_keys.shape[0]
    group_size = QH // KVH
    seq_count = lax.axis_size("seq")
    seq_index = lax.axis_index("seq")
    starts = jnp.cumsum(doc_lengths) - doc_lengths
    depth = min(seq_count, -(-(MOST - 1) // row_count) + 1)
    pad_rows = 8
    key_scale_row = jnp.repeat(key_scales.reshape(-1), BLK)
    value_scale_row = jnp.repeat(value_scales.reshape(-1), BLK)
    scale_rows = jnp.zeros((2, pad_rows, row_count), jnp.bfloat16)
    scale_rows = scale_rows.at[0, 0].set(key_scale_row).at[1, 0].set(value_scale_row)
    packet = jnp.concatenate([jnp.stack([local_keys.T, local_values]), scale_rows], axis=1)
    stages = gather_stages(packet, seq_count, depth)
    own_pos = seq_index * row_count + jnp.arange(row_count, dtype=jnp.int32)
    low = starts[doc_index(own_pos, starts)]
    used = jnp.clip(seq_index - low[0] // row_count + 1, 1, depth).astype(jnp.int32)
    low_tile = jnp.broadcast_to(low[:, None], (row_count, row_count)).astype(jnp.int32)
    mean = value_means.reshape(1, HD)
    query_all = queries.reshape(row_count, group_size, HD).transpose(1, 0, 2).reshape(-1, HD)
    chunks = [
        jnp.concatenate([stages[0]] + stages[1], axis=0),
        jnp.concatenate(stages[2], axis=0),
        jnp.concatenate(stages[3], axis=0),
    ]
    state = None
    offset = 0
    for index, chunk in enumerate(chunks):
        slots = chunk.shape[0]
        if slots % 2:
            chunk = jnp.concatenate([chunk, jnp.zeros((1,) + chunk.shape[1:], chunk.dtype)])
        pairs = jnp.clip((used - offset + 1) // 2, 0, chunk.shape[0] // 2).astype(jnp.int32)
        info = jnp.stack([seq_index.astype(jnp.int32), pairs, low[-1].astype(jnp.int32)])
        last = index == len(chunks) - 1
        state = attend_part(
            info, query_all, chunk, low_tile, mean, state, offset, last, queries.shape[1]
        )
        offset += slots
    return state


def solution(mesh):
    in_specs = (
        P("seq", "head"),
        P(("seq", "head"), None),
        P(("seq", "head"), None),
        P("seq", "head"),
        P("seq", "head"),
        P("head"),
        P(),
    )
    out_specs = P("seq", "head")
    return jax.shard_map(shards, mesh=mesh, in_specs=in_specs, out_specs=out_specs, check_vma=False)
```

```python
import functools
import math

import jax
import jax.numpy as jnp
from jax import lax
from jax.experimental import pallas as pl
from jax.experimental.pallas import tpu as pltpu
from jax.sharding import PartitionSpec as P

QH = 64
KVH = 8
HD = 128
BLK = 64
MOST = 5120

NEG = -1e30


def doc_index(positions, starts):
    return jnp.sum((starts[None, :] <= positions[:, None]).astype(jnp.int32), axis=1) - 1


def shift_from(x, offset, count):
    pairs = [(i, (i + offset) % count) for i in range(count)]
    return lax.ppermute(x, "seq", pairs)


def gather_stages(packet, count, depth):
    held = packet[None]
    stages = [held]
    for width, shifts in ((1, (1, 2, 3)), (4, (4, 8, 12)), (16, (16, 32))):
        parts = []
        for offset in shifts:
            need = min(width, depth - offset)
            if need > 0:
                parts.append(shift_from(held[:need], offset, count))
        stages.append(parts)
        held = jnp.concatenate([held] + parts, axis=0)
    return stages


def attention_kernel(first, last, offset, *refs):
    info_ref, query_ref, window_ref, low_ref, mean_ref = refs[:5]
    rest = refs[5:]
    if not first:
        max_in, sum_in, acc_in = rest[:3]
        rest = rest[3:]
    if last:
        out_ref = rest[0]
        rest = rest[1:]
    else:
        max_out, sum_out, acc_out = rest[:3]
        rest = rest[3:]
    max_ref, sum_ref, acc_ref = rest
    group_size, rows, _ = acc_ref.shape
    inv_scale = 1.0 / math.sqrt(HD)
    seq_index = info_ref[0]
    pairs = info_ref[1]
    if first:
        max_ref[...] = jnp.full(max_ref.shape, NEG, jnp.float32)
        sum_ref[...] = jnp.zeros(sum_ref.shape, jnp.float32)
        acc_ref[...] = jnp.zeros(acc_ref.shape, jnp.float32)
    else:
        max_ref[...] = max_in[...]
        sum_ref[...] = sum_in[...]
        acc_ref[...] = acc_in[...]
    query_pos = seq_index * rows + lax.broadcasted_iota(jnp.int32, (rows, rows), 0)
    low = low_ref[...]
    lane = lax.broadcasted_iota(jnp.int32, (rows, rows), 1)
    query_all = query_ref[...]

    low_top = info_ref[2]

    def fold_pair(pair, masked):
        parts = []
        for half in range(2):
            slot = 2 * pair + half
            key_t = window_ref[slot, 0, :HD, :]
            key_scale = window_ref[slot, 0, HD:HD + 1, :].astype(jnp.float32) * inv_scale
            value_scale = window_ref[slot, 1, rows:rows + 1, :].astype(jnp.float32)
            scores = jnp.dot(query_all, key_t, preferred_element_type=jnp.float32)
            scores = scores.reshape(group_size, rows, rows) * key_scale[None]
            allowed = None
            if masked:
                key_pos = (seq_index - offset - slot) * rows + lane
                allowed = ((key_pos <= query_pos) & (key_pos >= low))[None]
                scores = jnp.where(allowed, scores, NEG)
            parts.append((scores, allowed, value_scale[None], slot))
        run_max = max_ref[...][:, :, :1]
        both_max = jnp.maximum(parts[0][0], parts[1][0])
        new_max = jnp.maximum(run_max, jnp.max(both_max, axis=2, keepdims=True))
        factor = jnp.exp(run_max - new_max)
        acc = acc_ref[...] * factor
        weight_sum = None
        for scores, allowed, value_scale, slot in parts:
            weights = jnp.exp(scores - new_max)
            if masked:
                weights = jnp.where(allowed, weights, 0.0)
            weight_sum = weights if weight_sum is None else weight_sum + weights
            scaled = (weights * value_scale).astype(jnp.bfloat16).reshape(group_size * rows, rows)
            value_tile = window_ref[slot, 1, :rows, :]
            mixed = jnp.dot(scaled, value_tile, preferred_element_type=jnp.float32)
            acc = acc + mixed.reshape(group_size, rows, HD)
        run_sum = sum_ref[...][:, :, :1] * factor + jnp.sum(weight_sum, axis=2, keepdims=True)
        acc_ref[...] = acc
        max_ref[...] = jnp.broadcast_to(new_max, max_ref.shape)
        sum_ref[...] = jnp.broadcast_to(run_sum, sum_ref.shape)

    def one_pair(pair, carry):
        nearest = offset + 2 * pair
        inside = (nearest >= 1) & ((seq_index - nearest - 1) * rows >= low_top)
        lax.cond(inside, lambda: fold_pair(pair, False), lambda: fold_pair(pair, True))
        return carry

    lax.fori_loop(0, pairs, one_pair, 0)
    if last:
        result = acc_ref[...] / sum_ref[...] + mean_ref[...][None]
        for g in range(group_size):
            out_ref[:, g * HD:(g + 1) * HD] = result[g].astype(jnp.bfloat16)
    else:
        max_out[...] = max_ref[...]
        sum_out[...] = sum_ref[...]
        acc_out[...] = acc_ref[...]


def attend_part(info, query_all, window, low, mean, state, offset, last, width):
    group_size = query_all.shape[0] // HD
    rows = low.shape[0]
    full = lambda shape: pl.BlockSpec(shape, lambda i, info: (0,) * len(shape))
    state_shape = jax.ShapeDtypeStruct((group_size, rows, HD), jnp.float32)
    operands = [query_all, window, low, mean] + ([] if state is None else list(state))
    if last:
        out_shape = jax.ShapeDtypeStruct((rows, width), jnp.bfloat16)
        out_specs = full((rows, width))
    else:
        out_shape = (state_shape,) * 3
        out_specs = (full(state_shape.shape),) * 3
    kernel = functools.partial(attention_kernel, state is None, last, offset)
    return pl.pallas_call(
        kernel,
        out_shape=out_shape,
        grid_spec=pltpu.PrefetchScalarGridSpec(
            num_scalar_prefetch=1,
            grid=(1,),
            in_specs=[full(x.shape) for x in operands],
            out_specs=out_specs,
            scratch_shapes=[pltpu.VMEM((group_size, rows, HD), jnp.float32)] * 3,
        ),
    )(info, *operands)


def shards(queries, key_tokens, value_tokens, key_scales, value_scales, value_means, doc_lengths):
    heads = lax.axis_size("head")
    both = jnp.stack([key_tokens, value_tokens], axis=1)
    both = both.reshape(both.shape[0], 2, heads, -1)
    both = lax.all_to_all(both, "head", split_axis=2, concat_axis=0, tiled=True)
    local_keys = both[:, 0, 0]
    local_values = both[:, 1, 0]
    row_count = local_keys.shape[0]
    group_size = QH // KVH
    seq_count = lax.axis_size("seq")
    seq_index = lax.axis_index("seq")
    starts = jnp.cumsum(doc_lengths) - doc_lengths
    depth = min(seq_count, -(-(MOST - 1) // row_count) + 1)
    pad_rows = 8
    key_scale_row = jnp.repeat(key_scales.reshape(-1), BLK)
    value_scale_row = jnp.repeat(value_scales.reshape(-1), BLK)
    scale_rows = jnp.zeros((2, pad_rows, row_count), jnp.bfloat16)
    scale_rows = scale_rows.at[0, 0].set(key_scale_row).at[1, 0].set(value_scale_row)
    packet = jnp.concatenate([jnp.stack([local_keys.T, local_values]), scale_rows], axis=1)
    stages = gather_stages(packet, seq_count, depth)
    own_pos = seq_index * row_count + jnp.arange(row_count, dtype=jnp.int32)
    low = starts[doc_index(own_pos, starts)]
    used = jnp.clip(seq_index - low[0] // row_count + 1, 1, depth).astype(jnp.int32)
    low_tile = jnp.broadcast_to(low[:, None], (row_count, row_count)).astype(jnp.int32)
    mean = value_means.reshape(1, HD)
    query_all = queries.reshape(row_count, group_size, HD).transpose(1, 0, 2).reshape(-1, HD)
    chunks = [
        jnp.concatenate([stages[0]] + stages[1], axis=0),
        jnp.concatenate(stages[2], axis=0),
        jnp.concatenate(stages[3], axis=0),
    ]
    state = None
    offset = 0
    for index, chunk in enumerate(chunks):
        slots = chunk.shape[0]
        if slots % 2:
            chunk = jnp.concatenate([chunk, jnp.zeros((1,) + chunk.shape[1:], chunk.dtype)])
        pairs = jnp.clip((used - offset + 1) // 2, 0, chunk.shape[0] // 2).astype(jnp.int32)
        info = jnp.stack([seq_index.astype(jnp.int32), pairs, low[-1].astype(jnp.int32)])
        last = index == len(chunks) - 1
        state = attend_part(
            info, query_all, chunk, low_tile, mean, state, offset, last, queries.shape[1]
        )
        offset += slots
    return state


def solution(mesh):
    in_specs = (
        P("seq", "head"),
        P(("seq", "head"), None),
        P(("seq", "head"), None),
        P("seq", "head"),
        P("seq", "head"),
        P("head"),
        P(),
    )
    out_specs = P("seq", "head")
    return jax.shard_map(shards, mesh=mesh, in_specs=in_specs, out_specs=out_specs, check_vma=False)
```

```python
import functools
import math

import jax
import jax.numpy as jnp
from jax import lax
from jax.experimental import pallas as pl
from jax.experimental.pallas import tpu as pltpu
from jax.sharding import PartitionSpec as P

QH = 64
KVH = 8
HD = 128
BLK = 64
MOST = 5120

NEG = -1e30


def doc_index(positions, starts):
    return jnp.sum((starts[None, :] <= positions[:, None]).astype(jnp.int32), axis=1) - 1


def shift_from(x, offset, count):
    pairs = [(i, (i + offset) % count) for i in range(count)]
    return lax.ppermute(x, "seq", pairs)


def gather_stages(packet, count, depth):
    held = packet[None]
    stages = [held]
    for width, shifts in ((1, (1, 2, 3)), (4, (4, 8, 12)), (16, (16, 32))):
        parts = []
        for offset in shifts:
            need = min(width, depth - offset)
            if need > 0:
                parts.append(shift_from(held[:need], offset, count))
        stages.append(parts)
        held = jnp.concatenate([held] + parts, axis=0)
    return stages


def attention_kernel(first, last, offset, *refs):
    info_ref, query_ref, window_ref, low_ref, mean_ref = refs[:5]
    rest = refs[5:]
    if not first:
        max_in, sum_in, acc_in = rest[:3]
        rest = rest[3:]
    if last:
        out_ref = rest[0]
        rest = rest[1:]
    else:
        max_out, sum_out, acc_out = rest[:3]
        rest = rest[3:]
    max_ref, sum_ref, acc_ref = rest
    group_size, rows, _ = acc_ref.shape
    inv_scale = 1.0 / math.sqrt(HD)
    seq_index = info_ref[0]
    pairs = info_ref[1]
    if first:
        max_ref[...] = jnp.full(max_ref.shape, NEG, jnp.float32)
        sum_ref[...] = jnp.zeros(sum_ref.shape, jnp.float32)
        acc_ref[...] = jnp.zeros(acc_ref.shape, jnp.float32)
    else:
        max_ref[...] = max_in[...]
        sum_ref[...] = sum_in[...]
        acc_ref[...] = acc_in[...]
    query_pos = seq_index * rows + lax.broadcasted_iota(jnp.int32, (rows, rows), 0)
    low = low_ref[...]
    lane = lax.broadcasted_iota(jnp.int32, (rows, rows), 1)
    query_all = query_ref[...]

    low_top = info_ref[2]
    ones = jnp.ones((rows, HD), jnp.bfloat16)

    def fold_pair(pair, masked):
        parts = []
        for half in range(2):
            slot = 2 * pair + half
            key_t = window_ref[slot, 0, :HD, :]
            key_scale = window_ref[slot, 0, HD:HD + 1, :].astype(jnp.float32) * inv_scale
            value_scale = window_ref[slot, 1, rows:rows + 1, :].astype(jnp.float32)
            scores = jnp.dot(query_all, key_t, preferred_element_type=jnp.float32)
            scores = scores.reshape(group_size, rows, rows) * key_scale[None]
            allowed = None
            if masked:
                key_pos = (seq_index - offset - slot) * rows + lane
                allowed = ((key_pos <= query_pos) & (key_pos >= low))[None]
                scores = jnp.where(allowed, scores, NEG)
            parts.append((scores, allowed, value_scale[None], slot))
        run_max = max_ref[...][:, :, :1]
        new_max = run_max
        for scores, _, _, _ in parts:
            new_max = jnp.maximum(new_max, jnp.max(scores, axis=2, keepdims=True))
        factor = jnp.exp(run_max - new_max)
        run_sum = sum_ref[...] * factor
        acc = acc_ref[...] * factor
        for scores, allowed, value_scale, slot in parts:
            weights = jnp.exp(scores - new_max)
            if masked:
                weights = jnp.where(allowed, weights, 0.0)
            flat = weights.reshape(group_size * rows, rows)
            high = flat.astype(jnp.bfloat16)
            low_part = (flat - high.astype(jnp.float32)).astype(jnp.bfloat16)
            row_sum = jnp.dot(high, ones, preferred_element_type=jnp.float32) + jnp.dot(
                low_part, ones, preferred_element_type=jnp.float32
            )
            run_sum = run_sum + row_sum.reshape(group_size, rows, HD)
            scaled = (weights * value_scale).astype(jnp.bfloat16).reshape(group_size * rows, rows)
            value_tile = window_ref[slot, 1, :rows, :]
            mixed = jnp.dot(scaled, value_tile, preferred_element_type=jnp.float32)
            acc = acc + mixed.reshape(group_size, rows, HD)
        acc_ref[...] = acc
        max_ref[...] = jnp.broadcast_to(new_max, max_ref.shape)
        sum_ref[...] = run_sum

    def one_pair(pair, carry):
        nearest = offset + 2 * pair
        inside = (nearest >= 1) & ((seq_index - nearest - 1) * rows >= low_top)
        lax.cond(inside, lambda: fold_pair(pair, False), lambda: fold_pair(pair, True))
        return carry

    lax.fori_loop(0, pairs, one_pair, 0)
    if last:
        result = acc_ref[...] / sum_ref[...] + mean_ref[...][None]
        for g in range(group_size):
            out_ref[:, g * HD:(g + 1) * HD] = result[g].astype(jnp.bfloat16)
    else:
        max_out[...] = max_ref[...]
        sum_out[...] = sum_ref[...]
        acc_out[...] = acc_ref[...]


def attend_part(info, query_all, window, low, mean, state, offset, last, width):
    group_size = query_all.shape[0] // HD
    rows = low.shape[0]
    full = lambda shape: pl.BlockSpec(shape, lambda i, info: (0,) * len(shape))
    state_shape = jax.ShapeDtypeStruct((group_size, rows, HD), jnp.float32)
    operands = [query_all, window, low, mean] + ([] if state is None else list(state))
    if last:
        out_shape = jax.ShapeDtypeStruct((rows, width), jnp.bfloat16)
        out_specs = full((rows, width))
    else:
        out_shape = (state_shape,) * 3
        out_specs = (full(state_shape.shape),) * 3
    kernel = functools.partial(attention_kernel, state is None, last, offset)
    return pl.pallas_call(
        kernel,
        out_shape=out_shape,
        grid_spec=pltpu.PrefetchScalarGridSpec(
            num_scalar_prefetch=1,
            grid=(1,),
            in_specs=[full(x.shape) for x in operands],
            out_specs=out_specs,
            scratch_shapes=[pltpu.VMEM((group_size, rows, HD), jnp.float32)] * 3,
        ),
    )(info, *operands)


def shards(queries, key_tokens, value_tokens, key_scales, value_scales, value_means, doc_lengths):
    heads = lax.axis_size("head")
    both = jnp.stack([key_tokens, value_tokens], axis=1)
    both = both.reshape(both.shape[0], 2, heads, -1)
    both = lax.all_to_all(both, "head", split_axis=2, concat_axis=0, tiled=True)
    local_keys = both[:, 0, 0]
    local_values = both[:, 1, 0]
    row_count = local_keys.shape[0]
    group_size = QH // KVH
    seq_count = lax.axis_size("seq")
    seq_index = lax.axis_index("seq")
    starts = jnp.cumsum(doc_lengths) - doc_lengths
    depth = min(seq_count, -(-(MOST - 1) // row_count) + 1)
    pad_rows = 8
    key_scale_row = jnp.repeat(key_scales.reshape(-1), BLK)
    value_scale_row = jnp.repeat(value_scales.reshape(-1), BLK)
    scale_rows = jnp.zeros((2, pad_rows, row_count), jnp.bfloat16)
    scale_rows = scale_rows.at[0, 0].set(key_scale_row).at[1, 0].set(value_scale_row)
    packet = jnp.concatenate([jnp.stack([local_keys.T, local_values]), scale_rows], axis=1)
    stages = gather_stages(packet, seq_count, depth)
    own_pos = seq_index * row_count + jnp.arange(row_count, dtype=jnp.int32)
    low = starts[doc_index(own_pos, starts)]
    used = jnp.clip(seq_index - low[0] // row_count + 1, 1, depth).astype(jnp.int32)
    low_tile = jnp.broadcast_to(low[:, None], (row_count, row_count)).astype(jnp.int32)
    mean = value_means.reshape(1, HD)
    query_all = queries.reshape(row_count, group_size, HD).transpose(1, 0, 2).reshape(-1, HD)
    chunks = [
        jnp.concatenate([stages[0]] + stages[1], axis=0),
        jnp.concatenate(stages[2], axis=0),
        jnp.concatenate(stages[3], axis=0),
    ]
    state = None
    offset = 0
    for index, chunk in enumerate(chunks):
        slots = chunk.shape[0]
        if slots % 2:
            chunk = jnp.concatenate([chunk, jnp.zeros((1,) + chunk.shape[1:], chunk.dtype)])
        pairs = jnp.clip((used - offset + 1) // 2, 0, chunk.shape[0] // 2).astype(jnp.int32)
        info = jnp.stack([seq_index.astype(jnp.int32), pairs, low[-1].astype(jnp.int32)])
        last = index == len(chunks) - 1
        state = attend_part(
            info, query_all, chunk, low_tile, mean, state, offset, last, queries.shape[1]
        )
        offset += slots
    return state


def solution(mesh):
    in_specs = (
        P("seq", "head"),
        P(("seq", "head"), None),
        P(("seq", "head"), None),
        P("seq", "head"),
        P("seq", "head"),
        P("head"),
        P(),
    )
    out_specs = P("seq", "head")
    return jax.shard_map(shards, mesh=mesh, in_specs=in_specs, out_specs=out_specs, check_vma=False)
```

```python
import functools
import math

import jax
import jax.numpy as jnp
from jax import lax
from jax.experimental import pallas as pl
from jax.experimental.pallas import tpu as pltpu
from jax.sharding import PartitionSpec as P

QH = 64
KVH = 8
HD = 128
BLK = 64
MOST = 5120

NEG = -1e30


def doc_index(positions, starts):
    return jnp.sum((starts[None, :] <= positions[:, None]).astype(jnp.int32), axis=1) - 1


def shift_from(x, offset, count):
    pairs = [(i, (i + offset) % count) for i in range(count)]
    return lax.ppermute(x, "seq", pairs)


def gather_chunks(packet, count, depth):
    first = jnp.concatenate(
        [packet[None]] + [shift_from(packet[None], offset, count) for offset in (1, 2, 3)], axis=0
    )
    near = [shift_from(first, offset, count) for offset in (4, 8, 12)]
    far = [shift_from(first, offset, count) for offset in (16, 32)]
    block = jnp.concatenate([first] + near, axis=0)
    last = [shift_from(block[4:], 16, count), shift_from(block[4:depth - 32], 32, count)]
    pad = jnp.zeros((1,) + packet.shape, packet.dtype)
    return [
        (first, ((0, 0),)),
        (jnp.concatenate(near + far, axis=0), ((0, 4), (16, 16))),
        (jnp.concatenate(last + [pad], axis=0), ((0, 20), (12, 24))),
    ]


def attention_kernel(first, last, segments, *refs):
    info_ref, query_ref, window_ref, low_ref, mean_ref = refs[:5]
    rest = refs[5:]
    if not first:
        max_in, sum_in, acc_in = rest[:3]
        rest = rest[3:]
    if last:
        out_ref = rest[0]
        rest = rest[1:]
    else:
        max_out, sum_out, acc_out = rest[:3]
        rest = rest[3:]
    max_ref, sum_ref, acc_ref = rest
    group_size, rows, _ = acc_ref.shape
    inv_scale = 1.0 / math.sqrt(HD)
    seq_index = info_ref[0]
    used = info_ref[1]
    if first:
        max_ref[...] = jnp.full(max_ref.shape, NEG, jnp.float32)
        sum_ref[...] = jnp.zeros(sum_ref.shape, jnp.float32)
        acc_ref[...] = jnp.zeros(acc_ref.shape, jnp.float32)
    else:
        max_ref[...] = max_in[...]
        sum_ref[...] = sum_in[...]
        acc_ref[...] = acc_in[...]
    query_pos = seq_index * rows + lax.broadcasted_iota(jnp.int32, (rows, rows), 0)
    low = low_ref[...]
    lane = lax.broadcasted_iota(jnp.int32, (rows, rows), 1)
    query_all = query_ref[...]

    low_top = info_ref[2]

    def fold_pair(pair, shift, masked):
        parts = []
        for half in range(2):
            slot = 2 * pair + half
            key_t = window_ref[slot, 0, :HD, :]
            key_scale = window_ref[slot, 0, HD:HD + 1, :].astype(jnp.float32) * inv_scale
            value_scale = window_ref[slot, 1, rows:rows + 1, :].astype(jnp.float32)
            scores = jnp.dot(query_all, key_t, preferred_element_type=jnp.float32)
            scores = scores.reshape(group_size, rows, rows) * key_scale[None]
            allowed = None
            if masked:
                key_pos = (seq_index - shift - slot) * rows + lane
                allowed = ((key_pos <= query_pos) & (key_pos >= low))[None]
                scores = jnp.where(allowed, scores, NEG)
            parts.append((scores, allowed, value_scale[None], slot))
        run_max = max_ref[...][:, :, :1]
        new_max = run_max
        for scores, _, _, _ in parts:
            new_max = jnp.maximum(new_max, jnp.max(scores, axis=2, keepdims=True))
        factor = jnp.exp(run_max - new_max)
        run_sum = sum_ref[...][:, :, :1] * factor
        acc = acc_ref[...] * factor
        for scores, allowed, value_scale, slot in parts:
            weights = jnp.exp(scores - new_max)
            if masked:
                weights = jnp.where(allowed, weights, 0.0)
            run_sum = run_sum + jnp.sum(weights, axis=2, keepdims=True)
            scaled = (weights * value_scale).astype(jnp.bfloat16).reshape(group_size * rows, rows)
            value_tile = window_ref[slot, 1, :rows, :]
            mixed = jnp.dot(scaled, value_tile, preferred_element_type=jnp.float32)
            acc = acc + mixed.reshape(group_size, rows, HD)
        acc_ref[...] = acc
        max_ref[...] = jnp.broadcast_to(new_max, max_ref.shape)
        sum_ref[...] = jnp.broadcast_to(run_sum, sum_ref.shape)

    def one_pair(pair, carry):
        shift = jnp.int32(segments[0][1])
        for begin, moved in segments[1:]:
            shift = jnp.where(2 * pair >= begin, jnp.int32(moved), shift)
        nearest = shift + 2 * pair
        inside = (nearest >= 1) & ((seq_index - nearest - 1) * rows >= low_top)
        branch = jnp.where(nearest >= used, 0, jnp.where(inside, 1, 2))
        lax.switch(
            branch,
            [
                lambda: None,
                lambda: fold_pair(pair, shift, False),
                lambda: fold_pair(pair, shift, True),
            ],
        )
        return carry

    lax.fori_loop(0, window_ref.shape[0] // 2, one_pair, 0)
    if last:
        result = acc_ref[...] / sum_ref[...] + mean_ref[...][None]
        for g in range(group_size):
            out_ref[:, g * HD:(g + 1) * HD] = result[g].astype(jnp.bfloat16)
    else:
        max_out[...] = max_ref[...]
        sum_out[...] = sum_ref[...]
        acc_out[...] = acc_ref[...]


def attend_part(info, query_all, window, low, mean, state, segments, last, width):
    group_size = query_all.shape[0] // HD
    rows = low.shape[0]
    full = lambda shape: pl.BlockSpec(shape, lambda i, info: (0,) * len(shape))
    state_shape = jax.ShapeDtypeStruct((group_size, rows, HD), jnp.float32)
    operands = [query_all, window, low, mean] + ([] if state is None else list(state))
    if last:
        out_shape = jax.ShapeDtypeStruct((rows, width), jnp.bfloat16)
        out_specs = full((rows, width))
    else:
        out_shape = (state_shape,) * 3
        out_specs = (full(state_shape.shape),) * 3
    kernel = functools.partial(attention_kernel, state is None, last, segments)
    return pl.pallas_call(
        kernel,
        out_shape=out_shape,
        grid_spec=pltpu.PrefetchScalarGridSpec(
            num_scalar_prefetch=1,
            grid=(1,),
            in_specs=[full(x.shape) for x in operands],
            out_specs=out_specs,
            scratch_shapes=[pltpu.VMEM((group_size, rows, HD), jnp.float32)] * 3,
        ),
    )(info, *operands)


def shards(queries, key_tokens, value_tokens, key_scales, value_scales, value_means, doc_lengths):
    heads = lax.axis_size("head")
    both = jnp.stack([key_tokens, value_tokens], axis=1)
    both = both.reshape(both.shape[0], 2, heads, -1)
    both = lax.all_to_all(both, "head", split_axis=2, concat_axis=0, tiled=True)
    local_keys = both[:, 0, 0]
    local_values = both[:, 1, 0]
    row_count = local_keys.shape[0]
    group_size = QH // KVH
    seq_count = lax.axis_size("seq")
    seq_index = lax.axis_index("seq")
    starts = jnp.cumsum(doc_lengths) - doc_lengths
    depth = min(seq_count, -(-(MOST - 1) // row_count) + 1)
    pad_rows = 8
    key_scale_row = jnp.repeat(key_scales.reshape(-1), BLK)
    value_scale_row = jnp.repeat(value_scales.reshape(-1), BLK)
    scale_rows = jnp.zeros((2, pad_rows, row_count), jnp.bfloat16)
    scale_rows = scale_rows.at[0, 0].set(key_scale_row).at[1, 0].set(value_scale_row)
    packet = jnp.concatenate([jnp.stack([local_keys.T, local_values]), scale_rows], axis=1)
    chunks = gather_chunks(packet, seq_count, depth)
    own_pos = seq_index * row_count + jnp.arange(row_count, dtype=jnp.int32)
    low = starts[doc_index(own_pos, starts)]
    used = jnp.clip(seq_index - low[0] // row_count + 1, 1, depth).astype(jnp.int32)
    low_tile = jnp.broadcast_to(low[:, None], (row_count, row_count)).astype(jnp.int32)
    mean = value_means.reshape(1, HD)
    query_all = queries.reshape(row_count, group_size, HD).transpose(1, 0, 2).reshape(-1, HD)
    info = jnp.stack([seq_index.astype(jnp.int32), used, low[-1].astype(jnp.int32)])
    state = None
    for index, (chunk, segments) in enumerate(chunks):
        last = index == len(chunks) - 1
        state = attend_part(
            info, query_all, chunk, low_tile, mean, state, segments, last, queries.shape[1]
        )
    return state


def solution(mesh):
    in_specs = (
        P("seq", "head"),
        P(("seq", "head"), None),
        P(("seq", "head"), None),
        P("seq", "head"),
        P("seq", "head"),
        P("head"),
        P(),
    )
    out_specs = P("seq", "head")
    return jax.shard_map(shards, mesh=mesh, in_specs=in_specs, out_specs=out_specs, check_vma=False)
```

```python
import functools
import math

import jax
import jax.numpy as jnp
from jax import lax
from jax.experimental import pallas as pl
from jax.experimental.pallas import tpu as pltpu
from jax.sharding import PartitionSpec as P

QH = 64
KVH = 8
HD = 128
BLK = 64
MOST = 5120

NEG = -1e30


def doc_index(positions, starts):
    return jnp.sum((starts[None, :] <= positions[:, None]).astype(jnp.int32), axis=1) - 1


def shift_from(x, offset, count):
    pairs = [(i, (i + offset) % count) for i in range(count)]
    return lax.ppermute(x, "seq", pairs)


def gather_stages(packet, count, depth):
    held = packet[None]
    stages = [held]
    for width, shifts in ((1, (1, 2, 3)), (4, (4, 8, 12)), (16, (16, 32))):
        parts = []
        for offset in shifts:
            need = min(width, depth - offset)
            if need > 0:
                parts.append(shift_from(held[:need], offset, count))
        stages.append(parts)
        held = jnp.concatenate([held] + parts, axis=0)
    return stages


def attention_kernel(first, last, offset, *refs):
    info_ref, query_ref, window_ref, low_ref, mean_ref = refs[:5]
    rest = refs[5:]
    if not first:
        max_in, sum_in, acc_in = rest[:3]
        rest = rest[3:]
    if last:
        out_ref = rest[0]
        rest = rest[1:]
    else:
        max_out, sum_out, acc_out = rest[:3]
        rest = rest[3:]
    max_ref, sum_ref, acc_ref = rest
    group_size, rows = max_ref.shape
    inv_scale = 1.0 / math.sqrt(HD)
    seq_index = info_ref[0]
    pairs = info_ref[1]
    low_top = info_ref[2]
    if first:
        max_ref[...] = jnp.full(max_ref.shape, NEG, jnp.float32)
        sum_ref[...] = jnp.zeros(sum_ref.shape, jnp.float32)
        acc_ref[...] = jnp.zeros(acc_ref.shape, jnp.float32)
    else:
        max_ref[...] = max_in[...]
        sum_ref[...] = sum_in[...]
        acc_ref[...] = acc_in[...]
    query_pos = seq_index * rows + lax.broadcasted_iota(jnp.int32, (rows, rows), 1)
    low = jnp.broadcast_to(low_ref[0:1, :], (rows, rows))
    sub = lax.broadcasted_iota(jnp.int32, (rows, rows), 0)
    query_t = query_ref[...]

    def column(slot, part):
        row = window_ref[slot, part, rows:rows + 1, :].astype(jnp.float32)
        return jnp.transpose(jnp.broadcast_to(row, (rows, rows)))

    def fold_pair(pair, masked):
        parts = []
        for half in range(2):
            slot = 2 * pair + half
            key_tile = window_ref[slot, 0, :rows, :]
            scores = jnp.dot(key_tile, query_t, preferred_element_type=jnp.float32)
            key_scale = column(slot, 0) * inv_scale
            value_scale = column(slot, 1)
            allowed = None
            if masked:
                key_pos = (seq_index - offset - slot) * rows + sub
                allowed = (key_pos <= query_pos) & (key_pos >= low)
            blocks = []
            for g in range(group_size):
                block = scores[:, g * rows:(g + 1) * rows] * key_scale
                if masked:
                    block = jnp.where(allowed, block, NEG)
                blocks.append(block)
            parts.append((blocks, allowed, value_scale, slot))
        for g in range(group_size):
            run_max = max_ref[g:g + 1, :]
            new_max = run_max
            for blocks, _, _, _ in parts:
                new_max = jnp.maximum(new_max, jnp.max(blocks[g], axis=0, keepdims=True))
            factor = jnp.exp(run_max - new_max)
            run_sum = sum_ref[g:g + 1, :] * factor
            acc = acc_ref[:, g * rows:(g + 1) * rows] * factor
            for blocks, allowed, value_scale, slot in parts:
                weights = jnp.exp(blocks[g] - new_max)
                if masked:
                    weights = jnp.where(allowed, weights, 0.0)
                run_sum = run_sum + jnp.sum(weights, axis=0, keepdims=True)
                scaled = (weights * value_scale).astype(jnp.bfloat16)
                value_t = window_ref[slot, 1, :HD, :]
                acc = acc + jnp.dot(value_t, scaled, preferred_element_type=jnp.float32)
            acc_ref[:, g * rows:(g + 1) * rows] = acc
            max_ref[g:g + 1, :] = new_max
            sum_ref[g:g + 1, :] = run_sum

    def one_pair(pair, carry):
        nearest = offset + 2 * pair
        inside = (nearest >= 1) & ((seq_index - nearest - 1) * rows >= low_top)
        lax.cond(inside, lambda: fold_pair(pair, False), lambda: fold_pair(pair, True))
        return carry

    lax.fori_loop(0, pairs, one_pair, 0)
    if last:
        mean = mean_ref[...]
        for g in range(group_size):
            block = acc_ref[:, g * rows:(g + 1) * rows] / sum_ref[g:g + 1, :] + mean
            out_ref[:, g * HD:(g + 1) * HD] = jnp.transpose(block).astype(jnp.bfloat16)
    else:
        max_out[...] = max_ref[...]
        sum_out[...] = sum_ref[...]
        acc_out[...] = acc_ref[...]


def attend_part(info, query_t, window, low, mean, state, offset, last, width):
    group_size = query_t.shape[1] // HD
    rows = low.shape[1]
    full = lambda shape: pl.BlockSpec(shape, lambda i, info: (0,) * len(shape))
    row_shape = jax.ShapeDtypeStruct((group_size, rows), jnp.float32)
    acc_shape = jax.ShapeDtypeStruct((HD, group_size * rows), jnp.float32)
    operands = [query_t, window, low, mean] + ([] if state is None else list(state))
    if last:
        out_shape = jax.ShapeDtypeStruct((rows, width), jnp.bfloat16)
        out_specs = full((rows, width))
    else:
        out_shape = (row_shape, row_shape, acc_shape)
        out_specs = (full(row_shape.shape), full(row_shape.shape), full(acc_shape.shape))
    kernel = functools.partial(attention_kernel, state is None, last, offset)
    return pl.pallas_call(
        kernel,
        out_shape=out_shape,
        grid_spec=pltpu.PrefetchScalarGridSpec(
            num_scalar_prefetch=1,
            grid=(1,),
            in_specs=[full(x.shape) for x in operands],
            out_specs=out_specs,
            scratch_shapes=[
                pltpu.VMEM(row_shape.shape, jnp.float32),
                pltpu.VMEM(row_shape.shape, jnp.float32),
                pltpu.VMEM(acc_shape.shape, jnp.float32),
            ],
        ),
    )(info, *operands)


def shards(queries, key_tokens, value_tokens, key_scales, value_scales, value_means, doc_lengths):
    heads = lax.axis_size("head")
    both = jnp.stack([key_tokens, value_tokens], axis=1)
    both = both.reshape(both.shape[0], 2, heads, -1)
    both = lax.all_to_all(both, "head", split_axis=2, concat_axis=0, tiled=True)
    local_keys = both[:, 0, 0]
    local_values = both[:, 1, 0]
    row_count = local_keys.shape[0]
    group_size = QH // KVH
    seq_count = lax.axis_size("seq")
    seq_index = lax.axis_index("seq")
    starts = jnp.cumsum(doc_lengths) - doc_lengths
    depth = min(seq_count, -(-(MOST - 1) // row_count) + 1)
    pad_rows = 8
    key_scale_row = jnp.repeat(key_scales.reshape(-1), BLK)
    value_scale_row = jnp.repeat(value_scales.reshape(-1), BLK)
    scale_rows = jnp.zeros((2, pad_rows, row_count), jnp.bfloat16)
    scale_rows = scale_rows.at[0, 0].set(key_scale_row).at[1, 0].set(value_scale_row)
    packet = jnp.concatenate([jnp.stack([local_keys, local_values.T]), scale_rows], axis=1)
    stages = gather_stages(packet, seq_count, depth)
    own_pos = seq_index * row_count + jnp.arange(row_count, dtype=jnp.int32)
    low = starts[doc_index(own_pos, starts)]
    used = jnp.clip(seq_index - low[0] // row_count + 1, 1, depth).astype(jnp.int32)
    low_tile = jnp.broadcast_to(low[None, :], (8, row_count)).astype(jnp.int32)
    mean = jnp.broadcast_to(value_means.reshape(HD, 1), (HD, row_count))
    query_all = queries.reshape(row_count, group_size, HD).transpose(2, 1, 0).reshape(HD, -1)
    chunks = [
        jnp.concatenate([stages[0]] + stages[1], axis=0),
        jnp.concatenate(stages[2], axis=0),
        jnp.concatenate(stages[3], axis=0),
    ]
    state = None
    offset = 0
    for index, chunk in enumerate(chunks):
        slots = chunk.shape[0]
        if slots % 2:
            chunk = jnp.concatenate([chunk, jnp.zeros((1,) + chunk.shape[1:], chunk.dtype)])
        pairs = jnp.clip((used - offset + 1) // 2, 0, chunk.shape[0] // 2).astype(jnp.int32)
        info = jnp.stack([seq_index.astype(jnp.int32), pairs, low[-1].astype(jnp.int32)])
        last = index == len(chunks) - 1
        state = attend_part(
            info, query_all, chunk, low_tile, mean, state, offset, last, queries.shape[1]
        )
        offset += slots
    return state


def solution(mesh):
    in_specs = (
        P("seq", "head"),
        P(("seq", "head"), None),
        P(("seq", "head"), None),
        P("seq", "head"),
        P("seq", "head"),
        P("head"),
        P(),
    )
    out_specs = P("seq", "head")
    return jax.shard_map(shards, mesh=mesh, in_specs=in_specs, out_specs=out_specs, check_vma=False)
```

```python
import functools
import math

import jax
import jax.numpy as jnp
from jax import lax
from jax.experimental import pallas as pl
from jax.experimental.pallas import tpu as pltpu
from jax.sharding import PartitionSpec as P

QH = 64
KVH = 8
HD = 128
BLK = 64
MOST = 5120

NEG = -1e30


def doc_index(positions, starts):
    return jnp.sum((starts[None, :] <= positions[:, None]).astype(jnp.int32), axis=1) - 1


def shift_from(x, offset, count):
    pairs = [(i, (i + offset) % count) for i in range(count)]
    return lax.ppermute(x, "seq", pairs)


def gather_stages(packet, count, depth):
    first = [packet[None]] + [shift_from(packet[None], offset, count) for offset in (1, 2, 3)]
    block = jnp.concatenate(first, axis=0)
    middle = [shift_from(block, offset, count) for offset in (4, 8, 12, 16)]
    block = jnp.concatenate([block] + middle, axis=0)
    last = [shift_from(block[4:], 16, count), shift_from(block[4:depth - 32], 32, count)]
    return [first, middle, last]


def attention_kernel(first, last, offset, *refs):
    info_ref, query_ref, window_ref, low_ref, mean_ref = refs[:5]
    rest = refs[5:]
    if not first:
        max_in, sum_in, acc_in = rest[:3]
        rest = rest[3:]
    if last:
        out_ref = rest[0]
        rest = rest[1:]
    else:
        max_out, sum_out, acc_out = rest[:3]
        rest = rest[3:]
    max_ref, sum_ref, acc_ref = rest
    group_size, rows = max_ref.shape
    inv_scale = 1.0 / math.sqrt(HD)
    seq_index = info_ref[0]
    pairs = info_ref[1]
    low_top = info_ref[2]
    if first:
        max_ref[...] = jnp.full(max_ref.shape, NEG, jnp.float32)
        sum_ref[...] = jnp.zeros(sum_ref.shape, jnp.float32)
        acc_ref[...] = jnp.zeros(acc_ref.shape, jnp.float32)
    else:
        max_ref[...] = max_in[...]
        sum_ref[...] = sum_in[...]
        acc_ref[...] = acc_in[...]
    query_pos = seq_index * rows + lax.broadcasted_iota(jnp.int32, (rows, rows), 1)
    low = jnp.broadcast_to(low_ref[0:1, :], (rows, rows))
    sub = lax.broadcasted_iota(jnp.int32, (rows, rows), 0)
    query_t = query_ref[...]

    def column(slot, part):
        row = window_ref[slot, part, rows:rows + 1, :].astype(jnp.float32)
        return jnp.transpose(jnp.broadcast_to(row, (rows, rows)))

    def fold_pair(pair, masked):
        parts = []
        for half in range(2):
            slot = 2 * pair + half
            key_tile = window_ref[slot, 0, :rows, :]
            scores = jnp.dot(key_tile, query_t, preferred_element_type=jnp.float32)
            key_scale = column(slot, 0) * inv_scale
            value_scale = column(slot, 1)
            allowed = None
            if masked:
                key_pos = (seq_index - offset - slot) * rows + sub
                allowed = (key_pos <= query_pos) & (key_pos >= low)
            blocks = []
            for g in range(group_size):
                block = scores[:, g * rows:(g + 1) * rows] * key_scale
                if masked:
                    block = jnp.where(allowed, block, NEG)
                blocks.append(block)
            parts.append((blocks, allowed, value_scale, slot))
        for g in range(group_size):
            run_max = max_ref[g:g + 1, :]
            new_max = run_max
            for blocks, _, _, _ in parts:
                new_max = jnp.maximum(new_max, jnp.max(blocks[g], axis=0, keepdims=True))
            factor = jnp.exp(run_max - new_max)
            run_sum = sum_ref[g:g + 1, :] * factor
            acc = acc_ref[:, g * rows:(g + 1) * rows] * factor
            for blocks, allowed, value_scale, slot in parts:
                weights = jnp.exp(blocks[g] - new_max)
                if masked:
                    weights = jnp.where(allowed, weights, 0.0)
                run_sum = run_sum + jnp.sum(weights, axis=0, keepdims=True)
                scaled = (weights * value_scale).astype(jnp.bfloat16)
                value_t = window_ref[slot, 1, :HD, :]
                acc = acc + jnp.dot(value_t, scaled, preferred_element_type=jnp.float32)
            acc_ref[:, g * rows:(g + 1) * rows] = acc
            max_ref[g:g + 1, :] = new_max
            sum_ref[g:g + 1, :] = run_sum

    def one_pair(pair, carry):
        nearest = offset + 2 * pair
        inside = (nearest >= 1) & ((seq_index - nearest - 1) * rows >= low_top)
        lax.cond(inside, lambda: fold_pair(pair, False), lambda: fold_pair(pair, True))
        return carry

    lax.fori_loop(0, pairs, one_pair, 0)
    if last:
        mean = mean_ref[...]
        for g in range(group_size):
            block = acc_ref[:, g * rows:(g + 1) * rows] / sum_ref[g:g + 1, :] + mean
            out_ref[:, g * HD:(g + 1) * HD] = jnp.transpose(block).astype(jnp.bfloat16)
    else:
        max_out[...] = max_ref[...]
        sum_out[...] = sum_ref[...]
        acc_out[...] = acc_ref[...]


def attend_part(info, query_t, window, low, mean, state, offset, last, width):
    group_size = query_t.shape[1] // HD
    rows = low.shape[1]
    full = lambda shape: pl.BlockSpec(shape, lambda i, info: (0,) * len(shape))
    row_shape = jax.ShapeDtypeStruct((group_size, rows), jnp.float32)
    acc_shape = jax.ShapeDtypeStruct((HD, group_size * rows), jnp.float32)
    operands = [query_t, window, low, mean] + ([] if state is None else list(state))
    if last:
        out_shape = jax.ShapeDtypeStruct((rows, width), jnp.bfloat16)
        out_specs = full((rows, width))
    else:
        out_shape = (row_shape, row_shape, acc_shape)
        out_specs = (full(row_shape.shape), full(row_shape.shape), full(acc_shape.shape))
    kernel = functools.partial(attention_kernel, state is None, last, offset)
    return pl.pallas_call(
        kernel,
        out_shape=out_shape,
        grid_spec=pltpu.PrefetchScalarGridSpec(
            num_scalar_prefetch=1,
            grid=(1,),
            in_specs=[full(x.shape) for x in operands],
            out_specs=out_specs,
            scratch_shapes=[
                pltpu.VMEM(row_shape.shape, jnp.float32),
                pltpu.VMEM(row_shape.shape, jnp.float32),
                pltpu.VMEM(acc_shape.shape, jnp.float32),
            ],
        ),
    )(info, *operands)


def shards(queries, key_tokens, value_tokens, key_scales, value_scales, value_means, doc_lengths):
    heads = lax.axis_size("head")
    both = jnp.stack([key_tokens, value_tokens], axis=1)
    both = both.reshape(both.shape[0], 2, heads, -1)
    both = lax.all_to_all(both, "head", split_axis=2, concat_axis=0, tiled=True)
    local_keys = both[:, 0, 0]
    local_values = both[:, 1, 0]
    row_count = local_keys.shape[0]
    group_size = QH // KVH
    seq_count = lax.axis_size("seq")
    seq_index = lax.axis_index("seq")
    starts = jnp.cumsum(doc_lengths) - doc_lengths
    depth = min(seq_count, -(-(MOST - 1) // row_count) + 1)
    pad_rows = 8
    key_scale_row = jnp.repeat(key_scales.reshape(-1), BLK)
    value_scale_row = jnp.repeat(value_scales.reshape(-1), BLK)
    scale_rows = jnp.zeros((2, pad_rows, row_count), jnp.bfloat16)
    scale_rows = scale_rows.at[0, 0].set(key_scale_row).at[1, 0].set(value_scale_row)
    packet = jnp.concatenate([jnp.stack([local_keys, local_values.T]), scale_rows], axis=1)
    stages = gather_stages(packet, seq_count, depth)
    own_pos = seq_index * row_count + jnp.arange(row_count, dtype=jnp.int32)
    low = starts[doc_index(own_pos, starts)]
    used = jnp.clip(seq_index - low[0] // row_count + 1, 1, depth).astype(jnp.int32)
    low_tile = jnp.broadcast_to(low[None, :], (8, row_count)).astype(jnp.int32)
    mean = jnp.broadcast_to(value_means.reshape(HD, 1), (HD, row_count))
    query_all = queries.reshape(row_count, group_size, HD).transpose(2, 1, 0).reshape(HD, -1)
    chunks = [jnp.concatenate(stage, axis=0) for stage in stages]
    state = None
    offset = 0
    for index, chunk in enumerate(chunks):
        slots = chunk.shape[0]
        if slots % 2:
            chunk = jnp.concatenate([chunk, jnp.zeros((1,) + chunk.shape[1:], chunk.dtype)])
        pairs = jnp.clip((used - offset + 1) // 2, 0, chunk.shape[0] // 2).astype(jnp.int32)
        info = jnp.stack([seq_index.astype(jnp.int32), pairs, low[-1].astype(jnp.int32)])
        last = index == len(chunks) - 1
        state = attend_part(
            info, query_all, chunk, low_tile, mean, state, offset, last, queries.shape[1]
        )
        offset += slots
    return state


def solution(mesh):
    in_specs = (
        P("seq", "head"),
        P(("seq", "head"), None),
        P(("seq", "head"), None),
        P("seq", "head"),
        P("seq", "head"),
        P("head"),
        P(),
    )
    out_specs = P("seq", "head")
    return jax.shard_map(shards, mesh=mesh, in_specs=in_specs, out_specs=out_specs, check_vma=False)
```

```python
import functools
import math

import jax
import jax.numpy as jnp
from jax import lax
from jax.experimental import pallas as pl
from jax.experimental.pallas import tpu as pltpu
from jax.sharding import PartitionSpec as P

QH = 64
KVH = 8
HD = 128
BLK = 64
MOST = 5120

NEG = -1e30


def doc_index(positions, starts):
    return jnp.sum((starts[None, :] <= positions[:, None]).astype(jnp.int32), axis=1) - 1


def shift_from(x, offset, count):
    pairs = [(i, (i + offset) % count) for i in range(count)]
    return lax.ppermute(x, "seq", pairs)


def gather_chunks(packet, count, depth):
    first = [packet[None]] + [shift_from(packet[None], offset, count) for offset in (1, 2, 3)]
    block = jnp.concatenate(first, axis=0)
    middle = [shift_from(block, offset, count) for offset in (4, 8, 12, 16, 32)]
    near = jnp.concatenate([block] + middle[:3], axis=0)
    near, *middle[3:] = lax.optimization_barrier([near] + middle[3:])
    last = [shift_from(near[4:], 16, count), shift_from(near[4:depth - 32], 32, count)]
    pad = jnp.zeros((1,) + packet.shape, packet.dtype)
    return [
        (block, ((0, 0),)),
        (jnp.concatenate(middle, axis=0), ((0, 4), (16, 16))),
        (jnp.concatenate(last + [pad], axis=0), ((0, 20), (12, 24))),
    ]


def attention_kernel(first, last, segments, *refs):
    info_ref, query_ref, window_ref, low_ref, mean_ref = refs[:5]
    rest = refs[5:]
    if not first:
        max_in, sum_in, acc_in = rest[:3]
        rest = rest[3:]
    if last:
        out_ref = rest[0]
        rest = rest[1:]
    else:
        max_out, sum_out, acc_out = rest[:3]
        rest = rest[3:]
    max_ref, sum_ref, acc_ref = rest
    group_size, rows = max_ref.shape
    inv_scale = 1.0 / math.sqrt(HD)
    seq_index = info_ref[0]
    used = info_ref[1]
    low_top = info_ref[2]
    if first:
        max_ref[...] = jnp.full(max_ref.shape, NEG, jnp.float32)
        sum_ref[...] = jnp.zeros(sum_ref.shape, jnp.float32)
        acc_ref[...] = jnp.zeros(acc_ref.shape, jnp.float32)
    else:
        max_ref[...] = max_in[...]
        sum_ref[...] = sum_in[...]
        acc_ref[...] = acc_in[...]
    query_pos = seq_index * rows + lax.broadcasted_iota(jnp.int32, (rows, rows), 1)
    low = jnp.broadcast_to(low_ref[0:1, :], (rows, rows))
    sub = lax.broadcasted_iota(jnp.int32, (rows, rows), 0)
    query_t = query_ref[...]

    def column(slot, part):
        row = window_ref[slot, part, rows:rows + 1, :].astype(jnp.float32)
        return jnp.transpose(jnp.broadcast_to(row, (rows, rows)))

    def fold_pair(pair, shift, masked):
        parts = []
        for half in range(2):
            slot = 2 * pair + half
            key_tile = window_ref[slot, 0, :rows, :]
            scores = jnp.dot(key_tile, query_t, preferred_element_type=jnp.float32)
            key_scale = column(slot, 0) * inv_scale
            value_scale = column(slot, 1)
            allowed = None
            if masked:
                key_pos = (seq_index - shift - slot) * rows + sub
                allowed = (key_pos <= query_pos) & (key_pos >= low)
            blocks = []
            for g in range(group_size):
                block = scores[:, g * rows:(g + 1) * rows] * key_scale
                if masked:
                    block = jnp.where(allowed, block, NEG)
                blocks.append(block)
            parts.append((blocks, allowed, value_scale, slot))
        for g in range(group_size):
            run_max = max_ref[g:g + 1, :]
            new_max = run_max
            for blocks, _, _, _ in parts:
                new_max = jnp.maximum(new_max, jnp.max(blocks[g], axis=0, keepdims=True))
            factor = jnp.exp(run_max - new_max)
            run_sum = sum_ref[g:g + 1, :] * factor
            acc = acc_ref[:, g * rows:(g + 1) * rows] * factor
            for blocks, allowed, value_scale, slot in parts:
                weights = jnp.exp(blocks[g] - new_max)
                if masked:
                    weights = jnp.where(allowed, weights, 0.0)
                run_sum = run_sum + jnp.sum(weights, axis=0, keepdims=True)
                scaled = (weights * value_scale).astype(jnp.bfloat16)
                value_t = window_ref[slot, 1, :HD, :]
                acc = acc + jnp.dot(value_t, scaled, preferred_element_type=jnp.float32)
            acc_ref[:, g * rows:(g + 1) * rows] = acc
            max_ref[g:g + 1, :] = new_max
            sum_ref[g:g + 1, :] = run_sum

    def one_pair(pair, carry):
        shift = jnp.int32(segments[0][1])
        for begin, moved in segments[1:]:
            shift = jnp.where(2 * pair >= begin, jnp.int32(moved), shift)
        nearest = shift + 2 * pair
        inside = (nearest >= 1) & ((seq_index - nearest - 1) * rows >= low_top)
        branch = jnp.where(nearest >= used, 0, jnp.where(inside, 1, 2))
        lax.switch(
            branch,
            [
                lambda: None,
                lambda: fold_pair(pair, shift, False),
                lambda: fold_pair(pair, shift, True),
            ],
        )
        return carry

    lax.fori_loop(0, window_ref.shape[0] // 2, one_pair, 0)
    if last:
        mean = mean_ref[...]
        for g in range(group_size):
            block = acc_ref[:, g * rows:(g + 1) * rows] / sum_ref[g:g + 1, :] + mean
            out_ref[:, g * HD:(g + 1) * HD] = jnp.transpose(block).astype(jnp.bfloat16)
    else:
        max_out[...] = max_ref[...]
        sum_out[...] = sum_ref[...]
        acc_out[...] = acc_ref[...]


def attend_part(info, query_t, window, low, mean, state, segments, last, width):
    group_size = query_t.shape[1] // HD
    rows = low.shape[1]
    full = lambda shape: pl.BlockSpec(shape, lambda i, info: (0,) * len(shape))
    row_shape = jax.ShapeDtypeStruct((group_size, rows), jnp.float32)
    acc_shape = jax.ShapeDtypeStruct((HD, group_size * rows), jnp.float32)
    operands = [query_t, window, low, mean] + ([] if state is None else list(state))
    if last:
        out_shape = jax.ShapeDtypeStruct((rows, width), jnp.bfloat16)
        out_specs = full((rows, width))
    else:
        out_shape = (row_shape, row_shape, acc_shape)
        out_specs = (full(row_shape.shape), full(row_shape.shape), full(acc_shape.shape))
    kernel = functools.partial(attention_kernel, state is None, last, segments)
    return pl.pallas_call(
        kernel,
        out_shape=out_shape,
        grid_spec=pltpu.PrefetchScalarGridSpec(
            num_scalar_prefetch=1,
            grid=(1,),
            in_specs=[full(x.shape) for x in operands],
            out_specs=out_specs,
            scratch_shapes=[
                pltpu.VMEM(row_shape.shape, jnp.float32),
                pltpu.VMEM(row_shape.shape, jnp.float32),
                pltpu.VMEM(acc_shape.shape, jnp.float32),
            ],
        ),
    )(info, *operands)


def shards(queries, key_tokens, value_tokens, key_scales, value_scales, value_means, doc_lengths):
    heads = lax.axis_size("head")
    both = jnp.stack([key_tokens, value_tokens], axis=1)
    both = both.reshape(both.shape[0], 2, heads, -1)
    both = lax.all_to_all(both, "head", split_axis=2, concat_axis=0, tiled=True)
    local_keys = both[:, 0, 0]
    local_values = both[:, 1, 0]
    row_count = local_keys.shape[0]
    group_size = QH // KVH
    seq_count = lax.axis_size("seq")
    seq_index = lax.axis_index("seq")
    starts = jnp.cumsum(doc_lengths) - doc_lengths
    depth = min(seq_count, -(-(MOST - 1) // row_count) + 1)
    pad_rows = 8
    key_scale_row = jnp.repeat(key_scales.reshape(-1), BLK)
    value_scale_row = jnp.repeat(value_scales.reshape(-1), BLK)
    scale_rows = jnp.zeros((2, pad_rows, row_count), jnp.bfloat16)
    scale_rows = scale_rows.at[0, 0].set(key_scale_row).at[1, 0].set(value_scale_row)
    packet = jnp.concatenate([jnp.stack([local_keys, local_values.T]), scale_rows], axis=1)
    chunks = gather_chunks(packet, seq_count, depth)
    own_pos = seq_index * row_count + jnp.arange(row_count, dtype=jnp.int32)
    low = starts[doc_index(own_pos, starts)]
    used = jnp.clip(seq_index - low[0] // row_count + 1, 1, depth).astype(jnp.int32)
    low_tile = jnp.broadcast_to(low[None, :], (8, row_count)).astype(jnp.int32)
    mean = jnp.broadcast_to(value_means.reshape(HD, 1), (HD, row_count))
    query_all = queries.reshape(row_count, group_size, HD).transpose(2, 1, 0).reshape(HD, -1)
    info = jnp.stack([seq_index.astype(jnp.int32), used, low[-1].astype(jnp.int32)])
    state = None
    for index, (chunk, segments) in enumerate(chunks):
        last = index == len(chunks) - 1
        state = attend_part(
            info, query_all, chunk, low_tile, mean, state, segments, last, queries.shape[1]
        )
    return state


def solution(mesh):
    in_specs = (
        P("seq", "head"),
        P(("seq", "head"), None),
        P(("seq", "head"), None),
        P("seq", "head"),
        P("seq", "head"),
        P("head"),
        P(),
    )
    out_specs = P("seq", "head")
    return jax.shard_map(shards, mesh=mesh, in_specs=in_specs, out_specs=out_specs, check_vma=False)
```

```python
import functools
import math

import jax
import jax.numpy as jnp
from jax import lax
from jax.experimental import pallas as pl
from jax.experimental.pallas import tpu as pltpu
from jax.sharding import PartitionSpec as P

QH = 64
KVH = 8
HD = 128
BLK = 64
MOST = 5120

NEG = -1e30


def doc_index(positions, starts):
    return jnp.sum((starts[None, :] <= positions[:, None]).astype(jnp.int32), axis=1) - 1


def shift_from(x, offset, count):
    pairs = [(i, (i + offset) % count) for i in range(count)]
    return lax.ppermute(x, "seq", pairs)


def gather_stages(packet, count, depth):
    first = [packet[None]] + [shift_from(packet[None], offset, count) for offset in (1, 2, 3)]
    block = jnp.concatenate(first, axis=0)
    middle = [shift_from(block, offset, count) for offset in (4, 8, 12, 16)]
    block = jnp.concatenate([block] + middle, axis=0)
    last = [shift_from(block[4:], 16, count), shift_from(block[4:depth - 32], 32, count)]
    return [first, middle, last]


def attention_kernel(first, last, offset, *refs):
    info_ref, query_ref, window_ref, low_ref, mean_ref = refs[:5]
    rest = refs[5:]
    if not first:
        max_in, sum_in, acc_in = rest[:3]
        rest = rest[3:]
    if last:
        out_ref = rest[0]
        rest = rest[1:]
    else:
        max_out, sum_out, acc_out = rest[:3]
        rest = rest[3:]
    max_ref, sum_ref, acc_ref = rest
    group_size, rows = max_ref.shape
    inv_scale = 1.0 / math.sqrt(HD)
    seq_index = info_ref[0]
    pairs = info_ref[1]
    low_top = info_ref[2]
    if first:
        max_ref[...] = jnp.full(max_ref.shape, NEG, jnp.float32)
        sum_ref[...] = jnp.zeros(sum_ref.shape, jnp.float32)
        acc_ref[...] = jnp.zeros(acc_ref.shape, jnp.float32)
    else:
        max_ref[...] = max_in[...]
        sum_ref[...] = sum_in[...]
        acc_ref[...] = acc_in[...]
    query_pos = seq_index * rows + lax.broadcasted_iota(jnp.int32, (rows, rows), 1)
    low = jnp.broadcast_to(low_ref[0:1, :], (rows, rows))
    sub = lax.broadcasted_iota(jnp.int32, (rows, rows), 0)
    query_t = query_ref[...]

    def column(slot, part):
        row = window_ref[slot, part, rows:rows + 1, :].astype(jnp.float32)
        return jnp.transpose(jnp.broadcast_to(row, (rows, rows)))

    def fold_pair(pair, masked):
        parts = []
        for half in range(2):
            slot = 2 * pair + half
            key_tile = window_ref[slot, 0, :rows, :]
            scores = jnp.dot(key_tile, query_t, preferred_element_type=jnp.float32)
            key_scale = column(slot, 0) * inv_scale
            value_scale = column(slot, 1)
            allowed = None
            if masked:
                key_pos = (seq_index - offset - slot) * rows + sub
                allowed = (key_pos <= query_pos) & (key_pos >= low)
            blocks = []
            for g in range(group_size):
                block = scores[:, g * rows:(g + 1) * rows] * key_scale
                if masked:
                    block = jnp.where(allowed, block, NEG)
                blocks.append(block)
            parts.append((blocks, allowed, value_scale, slot))
        for g in range(group_size):
            run_max = max_ref[g:g + 1, :]
            new_max = run_max
            for blocks, _, _, _ in parts:
                new_max = jnp.maximum(new_max, jnp.max(blocks[g], axis=0, keepdims=True))
            factor = jnp.exp(run_max - new_max)
            run_sum = sum_ref[g:g + 1, :] * factor
            acc = acc_ref[:, g * rows:(g + 1) * rows] * factor
            for blocks, allowed, value_scale, slot in parts:
                weights = jnp.exp(blocks[g] - new_max)
                if masked:
                    weights = jnp.where(allowed, weights, 0.0)
                run_sum = run_sum + jnp.sum(weights, axis=0, keepdims=True)
                scaled = (weights * value_scale).astype(jnp.bfloat16)
                value_t = window_ref[slot, 1, :HD, :]
                acc = acc + jnp.dot(value_t, scaled, preferred_element_type=jnp.float32)
            acc_ref[:, g * rows:(g + 1) * rows] = acc
            max_ref[g:g + 1, :] = new_max
            sum_ref[g:g + 1, :] = run_sum

    def one_pair(pair, carry):
        nearest = offset + 2 * pair
        inside = (nearest >= 1) & ((seq_index - nearest - 1) * rows >= low_top)
        lax.cond(inside, lambda: fold_pair(pair, False), lambda: fold_pair(pair, True))
        return carry

    lax.fori_loop(0, pairs, one_pair, 0)
    if last:
        mean = mean_ref[...]
        for g in range(group_size):
            block = acc_ref[:, g * rows:(g + 1) * rows] / sum_ref[g:g + 1, :] + mean
            out_ref[:, g * HD:(g + 1) * HD] = jnp.transpose(block).astype(jnp.bfloat16)
    else:
        max_out[...] = max_ref[...]
        sum_out[...] = sum_ref[...]
        acc_out[...] = acc_ref[...]


def attend_part(info, query_t, window, low, mean, state, offset, last, width):
    group_size = query_t.shape[1] // HD
    rows = low.shape[1]
    full = lambda shape: pl.BlockSpec(shape, lambda i, info: (0,) * len(shape))
    row_shape = jax.ShapeDtypeStruct((group_size, rows), jnp.float32)
    acc_shape = jax.ShapeDtypeStruct((HD, group_size * rows), jnp.float32)
    operands = [query_t, window, low, mean] + ([] if state is None else list(state))
    if last:
        out_shape = jax.ShapeDtypeStruct((rows, width), jnp.bfloat16)
        out_specs = full((rows, width))
    else:
        out_shape = (row_shape, row_shape, acc_shape)
        out_specs = (full(row_shape.shape), full(row_shape.shape), full(acc_shape.shape))
    kernel = functools.partial(attention_kernel, state is None, last, offset)
    return pl.pallas_call(
        kernel,
        out_shape=out_shape,
        grid_spec=pltpu.PrefetchScalarGridSpec(
            num_scalar_prefetch=1,
            grid=(1,),
            in_specs=[full(x.shape) for x in operands],
            out_specs=out_specs,
            scratch_shapes=[
                pltpu.VMEM(row_shape.shape, jnp.float32),
                pltpu.VMEM(row_shape.shape, jnp.float32),
                pltpu.VMEM(acc_shape.shape, jnp.float32),
            ],
        ),
    )(info, *operands)


def shards(queries, key_tokens, value_tokens, key_scales, value_scales, value_means, doc_lengths):
    heads = lax.axis_size("head")
    rows_in = key_tokens.shape[0]
    both = jnp.concatenate([key_tokens, value_tokens], axis=0)
    both = lax.all_to_all(both, "head", split_axis=1, concat_axis=0, tiled=True)
    both = both.reshape(heads, 2, rows_in, HD)
    local_keys = both[:, 0].reshape(heads * rows_in, HD)
    local_values = both[:, 1].reshape(heads * rows_in, HD)
    row_count = local_keys.shape[0]
    group_size = QH // KVH
    seq_count = lax.axis_size("seq")
    seq_index = lax.axis_index("seq")
    starts = jnp.cumsum(doc_lengths) - doc_lengths
    depth = min(seq_count, -(-(MOST - 1) // row_count) + 1)
    pad_rows = 8
    key_scale_row = jnp.repeat(key_scales.reshape(-1), BLK)
    value_scale_row = jnp.repeat(value_scales.reshape(-1), BLK)
    scale_rows = jnp.zeros((2, pad_rows, row_count), jnp.bfloat16)
    scale_rows = scale_rows.at[0, 0].set(key_scale_row).at[1, 0].set(value_scale_row)
    packet = jnp.concatenate([jnp.stack([local_keys, local_values.T]), scale_rows], axis=1)
    stages = gather_stages(packet, seq_count, depth)
    own_pos = seq_index * row_count + jnp.arange(row_count, dtype=jnp.int32)
    low = starts[doc_index(own_pos, starts)]
    used = jnp.clip(seq_index - low[0] // row_count + 1, 1, depth).astype(jnp.int32)
    low_tile = jnp.broadcast_to(low[None, :], (8, row_count)).astype(jnp.int32)
    mean = jnp.broadcast_to(value_means.reshape(HD, 1), (HD, row_count))
    query_all = queries.reshape(row_count, group_size, HD).transpose(2, 1, 0).reshape(HD, -1)
    chunks = [jnp.concatenate(stage, axis=0) for stage in stages]
    state = None
    offset = 0
    for index, chunk in enumerate(chunks):
        slots = chunk.shape[0]
        if slots % 2:
            chunk = jnp.concatenate([chunk, jnp.zeros((1,) + chunk.shape[1:], chunk.dtype)])
        pairs = jnp.clip((used - offset + 1) // 2, 0, chunk.shape[0] // 2).astype(jnp.int32)
        info = jnp.stack([seq_index.astype(jnp.int32), pairs, low[-1].astype(jnp.int32)])
        last = index == len(chunks) - 1
        state = attend_part(
            info, query_all, chunk, low_tile, mean, state, offset, last, queries.shape[1]
        )
        offset += slots
    return state


def solution(mesh):
    in_specs = (
        P("seq", "head"),
        P(("seq", "head"), None),
        P(("seq", "head"), None),
        P("seq", "head"),
        P("seq", "head"),
        P("head"),
        P(),
    )
    out_specs = P("seq", "head")
    return jax.shard_map(shards, mesh=mesh, in_specs=in_specs, out_specs=out_specs, check_vma=False)
```

```python
import functools
import math

import jax
import jax.numpy as jnp
from jax import lax
from jax.experimental import pallas as pl
from jax.experimental.pallas import tpu as pltpu
from jax.sharding import PartitionSpec as P

QH = 64
KVH = 8
HD = 128
BLK = 64
MOST = 5120

NEG = -1e30
STEP = 4


def doc_index(positions, starts):
    return jnp.sum((starts[None, :] <= positions[:, None]).astype(jnp.int32), axis=1) - 1


def shift_from(x, offset, count):
    pairs = [(i, (i + offset) % count) for i in range(count)]
    return lax.ppermute(x, "seq", pairs)


def gather_stages(packet, count, depth):
    first = [packet[None]] + [shift_from(packet[None], offset, count) for offset in (1, 2, 3)]
    block = jnp.concatenate(first, axis=0)
    middle = [shift_from(block, offset, count) for offset in (4, 8, 12, 16)]
    block = jnp.concatenate([block] + middle, axis=0)
    last = [shift_from(block[4:], 16, count), shift_from(block[4:depth - 32], 32, count)]
    return [first, middle, last]


def attention_kernel(first, last, offset, *refs):
    info_ref, query_ref, window_ref, low_ref, mean_ref = refs[:5]
    rest = refs[5:]
    if not first:
        max_in, sum_in, acc_in = rest[:3]
        rest = rest[3:]
    if last:
        out_ref = rest[0]
        rest = rest[1:]
    else:
        max_out, sum_out, acc_out = rest[:3]
        rest = rest[3:]
    max_ref, sum_ref, acc_ref = rest
    group_size, rows = max_ref.shape
    inv_scale = 1.0 / math.sqrt(HD)
    seq_index = info_ref[0]
    pairs = info_ref[1]
    low_top = info_ref[2]
    if first:
        max_ref[...] = jnp.full(max_ref.shape, NEG, jnp.float32)
        sum_ref[...] = jnp.zeros(sum_ref.shape, jnp.float32)
        acc_ref[...] = jnp.zeros(acc_ref.shape, jnp.float32)
    else:
        max_ref[...] = max_in[...]
        sum_ref[...] = sum_in[...]
        acc_ref[...] = acc_in[...]
    query_pos = seq_index * rows + lax.broadcasted_iota(jnp.int32, (rows, rows), 1)
    low = jnp.broadcast_to(low_ref[0:1, :], (rows, rows))
    sub = lax.broadcasted_iota(jnp.int32, (rows, rows), 0)
    query_t = query_ref[...]

    def column(slot, part):
        row = window_ref[slot, part, rows:rows + 1, :].astype(jnp.float32)
        return jnp.transpose(jnp.broadcast_to(row, (rows, rows)))

    def fold_pair(pair, masked):
        parts = []
        for half in range(STEP):
            slot = STEP * pair + half
            key_tile = window_ref[slot, 0, :rows, :]
            scores = jnp.dot(key_tile, query_t, preferred_element_type=jnp.float32)
            key_scale = column(slot, 0) * inv_scale
            value_scale = column(slot, 1)
            allowed = None
            if masked:
                key_pos = (seq_index - offset - slot) * rows + sub
                allowed = (key_pos <= query_pos) & (key_pos >= low)
            blocks = []
            for g in range(group_size):
                block = scores[:, g * rows:(g + 1) * rows] * key_scale
                if masked:
                    block = jnp.where(allowed, block, NEG)
                blocks.append(block)
            parts.append((blocks, allowed, value_scale, slot))
        for g in range(group_size):
            run_max = max_ref[g:g + 1, :]
            new_max = run_max
            for blocks, _, _, _ in parts:
                new_max = jnp.maximum(new_max, jnp.max(blocks[g], axis=0, keepdims=True))
            factor = jnp.exp(run_max - new_max)
            run_sum = sum_ref[g:g + 1, :] * factor
            acc = acc_ref[:, g * rows:(g + 1) * rows] * factor
            for blocks, allowed, value_scale, slot in parts:
                weights = jnp.exp(blocks[g] - new_max)
                if masked:
                    weights = jnp.where(allowed, weights, 0.0)
                run_sum = run_sum + jnp.sum(weights, axis=0, keepdims=True)
                scaled = (weights * value_scale).astype(jnp.bfloat16)
                value_t = window_ref[slot, 1, :HD, :]
                acc = acc + jnp.dot(value_t, scaled, preferred_element_type=jnp.float32)
            acc_ref[:, g * rows:(g + 1) * rows] = acc
            max_ref[g:g + 1, :] = new_max
            sum_ref[g:g + 1, :] = run_sum

    def one_pair(pair, carry):
        nearest = offset + STEP * pair
        inside = (nearest >= 1) & ((seq_index - nearest - STEP + 1) * rows >= low_top)
        lax.cond(inside, lambda: fold_pair(pair, False), lambda: fold_pair(pair, True))
        return carry

    lax.fori_loop(0, pairs, one_pair, 0)
    if last:
        mean = mean_ref[...]
        for g in range(group_size):
            block = acc_ref[:, g * rows:(g + 1) * rows] / sum_ref[g:g + 1, :] + mean
            out_ref[:, g * HD:(g + 1) * HD] = jnp.transpose(block).astype(jnp.bfloat16)
    else:
        max_out[...] = max_ref[...]
        sum_out[...] = sum_ref[...]
        acc_out[...] = acc_ref[...]


def attend_part(info, query_t, window, low, mean, state, offset, last, width):
    group_size = query_t.shape[1] // HD
    rows = low.shape[1]
    full = lambda shape: pl.BlockSpec(shape, lambda i, info: (0,) * len(shape))
    row_shape = jax.ShapeDtypeStruct((group_size, rows), jnp.float32)
    acc_shape = jax.ShapeDtypeStruct((HD, group_size * rows), jnp.float32)
    operands = [query_t, window, low, mean] + ([] if state is None else list(state))
    if last:
        out_shape = jax.ShapeDtypeStruct((rows, width), jnp.bfloat16)
        out_specs = full((rows, width))
    else:
        out_shape = (row_shape, row_shape, acc_shape)
        out_specs = (full(row_shape.shape), full(row_shape.shape), full(acc_shape.shape))
    kernel = functools.partial(attention_kernel, state is None, last, offset)
    return pl.pallas_call(
        kernel,
        out_shape=out_shape,
        grid_spec=pltpu.PrefetchScalarGridSpec(
            num_scalar_prefetch=1,
            grid=(1,),
            in_specs=[full(x.shape) for x in operands],
            out_specs=out_specs,
            scratch_shapes=[
                pltpu.VMEM(row_shape.shape, jnp.float32),
                pltpu.VMEM(row_shape.shape, jnp.float32),
                pltpu.VMEM(acc_shape.shape, jnp.float32),
            ],
        ),
    )(info, *operands)


def shards(queries, key_tokens, value_tokens, key_scales, value_scales, value_means, doc_lengths):
    heads = lax.axis_size("head")
    rows_in = key_tokens.shape[0]
    both = jnp.concatenate([key_tokens, value_tokens], axis=0)
    both = lax.all_to_all(both, "head", split_axis=1, concat_axis=0, tiled=True)
    both = both.reshape(heads, 2, rows_in, HD)
    local_keys = both[:, 0].reshape(heads * rows_in, HD)
    local_values = both[:, 1].reshape(heads * rows_in, HD)
    row_count = local_keys.shape[0]
    group_size = QH // KVH
    seq_count = lax.axis_size("seq")
    seq_index = lax.axis_index("seq")
    starts = jnp.cumsum(doc_lengths) - doc_lengths
    depth = min(seq_count, -(-(MOST - 1) // row_count) + 1)
    pad_rows = 8
    key_scale_row = jnp.repeat(key_scales.reshape(-1), BLK)
    value_scale_row = jnp.repeat(value_scales.reshape(-1), BLK)
    scale_rows = jnp.zeros((2, pad_rows, row_count), jnp.bfloat16)
    scale_rows = scale_rows.at[0, 0].set(key_scale_row).at[1, 0].set(value_scale_row)
    packet = jnp.concatenate([jnp.stack([local_keys, local_values.T]), scale_rows], axis=1)
    stages = gather_stages(packet, seq_count, depth)
    own_pos = seq_index * row_count + jnp.arange(row_count, dtype=jnp.int32)
    low = starts[doc_index(own_pos, starts)]
    used = jnp.clip(seq_index - low[0] // row_count + 1, 1, depth).astype(jnp.int32)
    low_tile = jnp.broadcast_to(low[None, :], (8, row_count)).astype(jnp.int32)
    mean = jnp.broadcast_to(value_means.reshape(HD, 1), (HD, row_count))
    query_all = queries.reshape(row_count, group_size, HD).transpose(2, 1, 0).reshape(HD, -1)
    chunks = [jnp.concatenate(stage, axis=0) for stage in stages]
    state = None
    offset = 0
    for index, chunk in enumerate(chunks):
        slots = chunk.shape[0]
        if slots % STEP:
            fill = STEP - slots % STEP
            chunk = jnp.concatenate([chunk, jnp.zeros((fill,) + chunk.shape[1:], chunk.dtype)])
        pairs = jnp.clip((used - offset + STEP - 1) // STEP, 0, chunk.shape[0] // STEP)
        pairs = pairs.astype(jnp.int32)
        info = jnp.stack([seq_index.astype(jnp.int32), pairs, low[-1].astype(jnp.int32)])
        last = index == len(chunks) - 1
        state = attend_part(
            info, query_all, chunk, low_tile, mean, state, offset, last, queries.shape[1]
        )
        offset += slots
    return state


def solution(mesh):
    in_specs = (
        P("seq", "head"),
        P(("seq", "head"), None),
        P(("seq", "head"), None),
        P("seq", "head"),
        P("seq", "head"),
        P("head"),
        P(),
    )
    out_specs = P("seq", "head")
    return jax.shard_map(shards, mesh=mesh, in_specs=in_specs, out_specs=out_specs, check_vma=False)
```

```python
import functools
import math

import jax
import jax.numpy as jnp
from jax import lax
from jax.experimental import pallas as pl
from jax.experimental.pallas import tpu as pltpu
from jax.sharding import PartitionSpec as P

QH = 64
KVH = 8
HD = 128
BLK = 64
MOST = 5120

NEG = -1e30


def doc_index(positions, starts):
    return jnp.sum((starts[None, :] <= positions[:, None]).astype(jnp.int32), axis=1) - 1


def shift_from(x, offset, count):
    pairs = [(i, (i + offset) % count) for i in range(count)]
    return lax.ppermute(x, "seq", pairs)


def gather_stages(packet, count, depth):
    first = [packet[None]] + [shift_from(packet[None], offset, count) for offset in (1, 2, 3)]
    block = jnp.concatenate(first, axis=0)
    middle = [
        shift_from(block, 4, count),
        shift_from(block[:2], 8, count),
        shift_from(block[:2], 10, count),
        shift_from(block, 12, count),
        shift_from(block, 16, count),
    ]
    block = jnp.concatenate([block] + middle, axis=0)
    last = [shift_from(block[4:], 16, count), shift_from(block[4:depth - 32], 32, count)]
    return [first, middle, last]


def attention_kernel(first, last, offset, *refs):
    info_ref, query_ref, window_ref, low_ref, mean_ref = refs[:5]
    rest = refs[5:]
    if not first:
        max_in, sum_in, acc_in = rest[:3]
        rest = rest[3:]
    if last:
        out_ref = rest[0]
        rest = rest[1:]
    else:
        max_out, sum_out, acc_out = rest[:3]
        rest = rest[3:]
    max_ref, sum_ref, acc_ref = rest
    group_size, rows = max_ref.shape
    inv_scale = 1.0 / math.sqrt(HD)
    seq_index = info_ref[0]
    pairs = info_ref[1]
    low_top = info_ref[2]
    if first:
        max_ref[...] = jnp.full(max_ref.shape, NEG, jnp.float32)
        sum_ref[...] = jnp.zeros(sum_ref.shape, jnp.float32)
        acc_ref[...] = jnp.zeros(acc_ref.shape, jnp.float32)
    else:
        max_ref[...] = max_in[...]
        sum_ref[...] = sum_in[...]
        acc_ref[...] = acc_in[...]
    query_pos = seq_index * rows + lax.broadcasted_iota(jnp.int32, (rows, rows), 1)
    low = jnp.broadcast_to(low_ref[0:1, :], (rows, rows))
    sub = lax.broadcasted_iota(jnp.int32, (rows, rows), 0)
    query_t = query_ref[...]

    def column(slot, part):
        row = window_ref[slot, part, rows:rows + 1, :].astype(jnp.float32)
        return jnp.transpose(jnp.broadcast_to(row, (rows, rows)))

    def fold_pair(pair, masked):
        parts = []
        for half in range(2):
            slot = 2 * pair + half
            key_tile = window_ref[slot, 0, :rows, :]
            scores = jnp.dot(key_tile, query_t, preferred_element_type=jnp.float32)
            key_scale = column(slot, 0) * inv_scale
            value_scale = column(slot, 1)
            allowed = None
            if masked:
                key_pos = (seq_index - offset - slot) * rows + sub
                allowed = (key_pos <= query_pos) & (key_pos >= low)
            blocks = []
            for g in range(group_size):
                block = scores[:, g * rows:(g + 1) * rows] * key_scale
                if masked:
                    block = jnp.where(allowed, block, NEG)
                blocks.append(block)
            parts.append((blocks, allowed, value_scale, slot))
        for g in range(group_size):
            run_max = max_ref[g:g + 1, :]
            new_max = run_max
            for blocks, _, _, _ in parts:
                new_max = jnp.maximum(new_max, jnp.max(blocks[g], axis=0, keepdims=True))
            factor = jnp.exp(run_max - new_max)
            run_sum = sum_ref[g:g + 1, :] * factor
            acc = acc_ref[:, g * rows:(g + 1) * rows] * factor
            for blocks, allowed, value_scale, slot in parts:
                weights = jnp.exp(blocks[g] - new_max)
                if masked:
                    weights = jnp.where(allowed, weights, 0.0)
                run_sum = run_sum + jnp.sum(weights, axis=0, keepdims=True)
                scaled = (weights * value_scale).astype(jnp.bfloat16)
                value_t = window_ref[slot, 1, :HD, :]
                acc = acc + jnp.dot(value_t, scaled, preferred_element_type=jnp.float32)
            acc_ref[:, g * rows:(g + 1) * rows] = acc
            max_ref[g:g + 1, :] = new_max
            sum_ref[g:g + 1, :] = run_sum

    def one_pair(pair, carry):
        nearest = offset + 2 * pair
        inside = (nearest >= 1) & ((seq_index - nearest - 1) * rows >= low_top)
        lax.cond(inside, lambda: fold_pair(pair, False), lambda: fold_pair(pair, True))
        return carry

    lax.fori_loop(0, pairs, one_pair, 0)
    if last:
        mean = mean_ref[...]
        for g in range(group_size):
            block = acc_ref[:, g * rows:(g + 1) * rows] / sum_ref[g:g + 1, :] + mean
            out_ref[:, g * HD:(g + 1) * HD] = jnp.transpose(block).astype(jnp.bfloat16)
    else:
        max_out[...] = max_ref[...]
        sum_out[...] = sum_ref[...]
        acc_out[...] = acc_ref[...]


def attend_part(info, query_t, window, low, mean, state, offset, last, width):
    group_size = query_t.shape[1] // HD
    rows = low.shape[1]
    full = lambda shape: pl.BlockSpec(shape, lambda i, info: (0,) * len(shape))
    row_shape = jax.ShapeDtypeStruct((group_size, rows), jnp.float32)
    acc_shape = jax.ShapeDtypeStruct((HD, group_size * rows), jnp.float32)
    operands = [query_t, window, low, mean] + ([] if state is None else list(state))
    if last:
        out_shape = jax.ShapeDtypeStruct((rows, width), jnp.bfloat16)
        out_specs = full((rows, width))
    else:
        out_shape = (row_shape, row_shape, acc_shape)
        out_specs = (full(row_shape.shape), full(row_shape.shape), full(acc_shape.shape))
    kernel = functools.partial(attention_kernel, state is None, last, offset)
    return pl.pallas_call(
        kernel,
        out_shape=out_shape,
        grid_spec=pltpu.PrefetchScalarGridSpec(
            num_scalar_prefetch=1,
            grid=(1,),
            in_specs=[full(x.shape) for x in operands],
            out_specs=out_specs,
            scratch_shapes=[
                pltpu.VMEM(row_shape.shape, jnp.float32),
                pltpu.VMEM(row_shape.shape, jnp.float32),
                pltpu.VMEM(acc_shape.shape, jnp.float32),
            ],
        ),
    )(info, *operands)


def shards(queries, key_tokens, value_tokens, key_scales, value_scales, value_means, doc_lengths):
    heads = lax.axis_size("head")
    rows_in = key_tokens.shape[0]
    both = jnp.concatenate([key_tokens, value_tokens], axis=0)
    both = lax.all_to_all(both, "head", split_axis=1, concat_axis=0, tiled=True)
    both = both.reshape(heads, 2, rows_in, HD)
    local_keys = both[:, 0].reshape(heads * rows_in, HD)
    local_values = both[:, 1].reshape(heads * rows_in, HD)
    row_count = local_keys.shape[0]
    group_size = QH // KVH
    seq_count = lax.axis_size("seq")
    seq_index = lax.axis_index("seq")
    starts = jnp.cumsum(doc_lengths) - doc_lengths
    depth = min(seq_count, -(-(MOST - 1) // row_count) + 1)
    pad_rows = 8
    key_scale_row = jnp.repeat(key_scales.reshape(-1), BLK)
    value_scale_row = jnp.repeat(value_scales.reshape(-1), BLK)
    scale_rows = jnp.zeros((2, pad_rows, row_count), jnp.bfloat16)
    scale_rows = scale_rows.at[0, 0].set(key_scale_row).at[1, 0].set(value_scale_row)
    packet = jnp.concatenate([jnp.stack([local_keys, local_values.T]), scale_rows], axis=1)
    stages = gather_stages(packet, seq_count, depth)
    own_pos = seq_index * row_count + jnp.arange(row_count, dtype=jnp.int32)
    low = starts[doc_index(own_pos, starts)]
    used = jnp.clip(seq_index - low[0] // row_count + 1, 1, depth).astype(jnp.int32)
    low_tile = jnp.broadcast_to(low[None, :], (8, row_count)).astype(jnp.int32)
    mean = jnp.broadcast_to(value_means.reshape(HD, 1), (HD, row_count))
    query_all = queries.reshape(row_count, group_size, HD).transpose(2, 1, 0).reshape(HD, -1)
    chunks = [jnp.concatenate(stage, axis=0) for stage in stages]
    state = None
    offset = 0
    for index, chunk in enumerate(chunks):
        slots = chunk.shape[0]
        if slots % 2:
            chunk = jnp.concatenate([chunk, jnp.zeros((1,) + chunk.shape[1:], chunk.dtype)])
        pairs = jnp.clip((used - offset + 1) // 2, 0, chunk.shape[0] // 2).astype(jnp.int32)
        info = jnp.stack([seq_index.astype(jnp.int32), pairs, low[-1].astype(jnp.int32)])
        last = index == len(chunks) - 1
        state = attend_part(
            info, query_all, chunk, low_tile, mean, state, offset, last, queries.shape[1]
        )
        offset += slots
    return state


def solution(mesh):
    in_specs = (
        P("seq", "head"),
        P(("seq", "head"), None),
        P(("seq", "head"), None),
        P("seq", "head"),
        P("seq", "head"),
        P("head"),
        P(),
    )
    out_specs = P("seq", "head")
    return jax.shard_map(shards, mesh=mesh, in_specs=in_specs, out_specs=out_specs, check_vma=False)
```

```python
import functools
import math

import jax
import jax.numpy as jnp
from jax import lax
from jax.experimental import pallas as pl
from jax.experimental.pallas import tpu as pltpu
from jax.sharding import PartitionSpec as P

QH = 64
KVH = 8
HD = 128
BLK = 64
MOST = 5120

NEG = -1e30


def doc_index(positions, starts):
    return jnp.sum((starts[None, :] <= positions[:, None]).astype(jnp.int32), axis=1) - 1


def shift_from(x, offset, count):
    pairs = [(i, (i + offset) % count) for i in range(count)]
    return lax.ppermute(x, "seq", pairs)


def gather_stages(packet, count, depth):
    first = [packet[None]] + [shift_from(packet[None], offset, count) for offset in (1, 2, 3)]
    block = jnp.concatenate(first, axis=0)
    middle = [shift_from(block, offset, count) for offset in (4, 8, 12, 16)]
    block = jnp.concatenate([block] + middle, axis=0)
    last = [shift_from(block[4:], 16, count), shift_from(block[4:depth - 32], 32, count)]
    return [first, middle, last]


def attention_kernel(first, last, layout, *refs):
    count = len(layout)
    info_ref, query_ref = refs[:2]
    windows = refs[2:2 + count]
    low_ref, mean_ref = refs[2 + count:4 + count]
    rest = refs[4 + count:]
    if not first:
        max_in, sum_in, acc_in = rest[:3]
        rest = rest[3:]
    if last:
        out_ref = rest[0]
        rest = rest[1:]
    else:
        max_out, sum_out, acc_out = rest[:3]
        rest = rest[3:]
    max_ref, sum_ref, acc_ref = rest
    group_size, rows = max_ref.shape
    inv_scale = 1.0 / math.sqrt(HD)
    seq_index = info_ref[0]
    used = info_ref[1]
    low_top = info_ref[2]
    if first:
        max_ref[...] = jnp.full(max_ref.shape, NEG, jnp.float32)
        sum_ref[...] = jnp.zeros(sum_ref.shape, jnp.float32)
        acc_ref[...] = jnp.zeros(acc_ref.shape, jnp.float32)
    else:
        max_ref[...] = max_in[...]
        sum_ref[...] = sum_in[...]
        acc_ref[...] = acc_in[...]
    query_pos = seq_index * rows + lax.broadcasted_iota(jnp.int32, (rows, rows), 1)
    low = jnp.broadcast_to(low_ref[0:1, :], (rows, rows))
    sub = lax.broadcasted_iota(jnp.int32, (rows, rows), 0)
    query_t = query_ref[...]

    def column(window_ref, slot, part):
        row = window_ref[slot, part, rows:rows + 1, :].astype(jnp.float32)
        return jnp.transpose(jnp.broadcast_to(row, (rows, rows)))

    def fold_pair(window_ref, offset, step, pair, masked):
        parts = []
        for half in range(step):
            slot = step * pair + half
            key_tile = window_ref[slot, 0, :rows, :]
            scores = jnp.dot(key_tile, query_t, preferred_element_type=jnp.float32)
            key_scale = column(window_ref, slot, 0) * inv_scale
            value_scale = column(window_ref, slot, 1)
            allowed = None
            if masked:
                key_pos = (seq_index - offset - slot) * rows + sub
                allowed = (key_pos <= query_pos) & (key_pos >= low)
            blocks = []
            for g in range(group_size):
                block = scores[:, g * rows:(g + 1) * rows] * key_scale
                if masked:
                    block = jnp.where(allowed, block, NEG)
                blocks.append(block)
            parts.append((blocks, allowed, value_scale, slot))
        for g in range(group_size):
            run_max = max_ref[g:g + 1, :]
            new_max = run_max
            for blocks, _, _, _ in parts:
                new_max = jnp.maximum(new_max, jnp.max(blocks[g], axis=0, keepdims=True))
            factor = jnp.exp(run_max - new_max)
            run_sum = sum_ref[g:g + 1, :] * factor
            acc = acc_ref[:, g * rows:(g + 1) * rows] * factor
            for blocks, allowed, value_scale, slot in parts:
                weights = jnp.exp(blocks[g] - new_max)
                if masked:
                    weights = jnp.where(allowed, weights, 0.0)
                run_sum = run_sum + jnp.sum(weights, axis=0, keepdims=True)
                scaled = (weights * value_scale).astype(jnp.bfloat16)
                value_t = window_ref[slot, 1, :HD, :]
                acc = acc + jnp.dot(value_t, scaled, preferred_element_type=jnp.float32)
            acc_ref[:, g * rows:(g + 1) * rows] = acc
            max_ref[g:g + 1, :] = new_max
            sum_ref[g:g + 1, :] = run_sum

    for window_ref, (offset, step) in zip(windows, layout):

        def one_step(pair, carry, window_ref=window_ref, offset=offset, step=step):
            nearest = offset + step * pair
            inside = (nearest >= 1) & ((seq_index - nearest - step + 1) * rows >= low_top)
            lax.cond(
                inside,
                lambda: fold_pair(window_ref, offset, step, pair, False),
                lambda: fold_pair(window_ref, offset, step, pair, True),
            )
            return carry

        reach = jnp.minimum(jnp.maximum(used - offset, 0), window_ref.shape[0])
        lax.fori_loop(0, (reach + step - 1) // step, one_step, 0)
    if last:
        mean = mean_ref[...]
        for g in range(group_size):
            block = acc_ref[:, g * rows:(g + 1) * rows] / sum_ref[g:g + 1, :] + mean
            out_ref[:, g * HD:(g + 1) * HD] = jnp.transpose(block).astype(jnp.bfloat16)
    else:
        max_out[...] = max_ref[...]
        sum_out[...] = sum_ref[...]
        acc_out[...] = acc_ref[...]


def attend_part(info, query_t, windows, layout, low, mean, state, last, width):
    group_size = query_t.shape[1] // HD
    rows = low.shape[1]
    full = lambda shape: pl.BlockSpec(shape, lambda i, info: (0,) * len(shape))
    row_shape = jax.ShapeDtypeStruct((group_size, rows), jnp.float32)
    acc_shape = jax.ShapeDtypeStruct((HD, group_size * rows), jnp.float32)
    operands = [query_t] + list(windows) + [low, mean] + ([] if state is None else list(state))
    if last:
        out_shape = jax.ShapeDtypeStruct((rows, width), jnp.bfloat16)
        out_specs = full((rows, width))
    else:
        out_shape = (row_shape, row_shape, acc_shape)
        out_specs = (full(row_shape.shape), full(row_shape.shape), full(acc_shape.shape))
    kernel = functools.partial(attention_kernel, state is None, last, layout)
    return pl.pallas_call(
        kernel,
        out_shape=out_shape,
        grid_spec=pltpu.PrefetchScalarGridSpec(
            num_scalar_prefetch=1,
            grid=(1,),
            in_specs=[full(x.shape) for x in operands],
            out_specs=out_specs,
            scratch_shapes=[
                pltpu.VMEM(row_shape.shape, jnp.float32),
                pltpu.VMEM(row_shape.shape, jnp.float32),
                pltpu.VMEM(acc_shape.shape, jnp.float32),
            ],
        ),
    )(info, *operands)


def shards(queries, key_tokens, value_tokens, key_scales, value_scales, value_means, doc_lengths):
    heads = lax.axis_size("head")
    rows_in = key_tokens.shape[0]
    both = jnp.concatenate([key_tokens, value_tokens], axis=0)
    both = lax.all_to_all(both, "head", split_axis=1, concat_axis=0, tiled=True)
    both = both.reshape(heads, 2, rows_in, HD)
    local_keys = both[:, 0].reshape(heads * rows_in, HD)
    local_values = both[:, 1].reshape(heads * rows_in, HD)
    row_count = local_keys.shape[0]
    group_size = QH // KVH
    seq_count = lax.axis_size("seq")
    seq_index = lax.axis_index("seq")
    starts = jnp.cumsum(doc_lengths) - doc_lengths
    depth = min(seq_count, -(-(MOST - 1) // row_count) + 1)
    pad_rows = 8
    key_scale_row = jnp.repeat(key_scales.reshape(-1), BLK)
    value_scale_row = jnp.repeat(value_scales.reshape(-1), BLK)
    scale_rows = jnp.zeros((2, pad_rows, row_count), jnp.bfloat16)
    scale_rows = scale_rows.at[0, 0].set(key_scale_row).at[1, 0].set(value_scale_row)
    packet = jnp.concatenate([jnp.stack([local_keys, local_values.T]), scale_rows], axis=1)
    stages = gather_stages(packet, seq_count, depth)
    own_pos = seq_index * row_count + jnp.arange(row_count, dtype=jnp.int32)
    low = starts[doc_index(own_pos, starts)]
    used = jnp.clip(seq_index - low[0] // row_count + 1, 1, depth).astype(jnp.int32)
    low_tile = jnp.broadcast_to(low[None, :], (8, row_count)).astype(jnp.int32)
    mean = jnp.broadcast_to(value_means.reshape(HD, 1), (HD, row_count))
    query_all = queries.reshape(row_count, group_size, HD).transpose(2, 1, 0).reshape(HD, -1)
    info = jnp.stack([seq_index.astype(jnp.int32), used, low[-1].astype(jnp.int32)])
    first, middle, final = stages
    near, far = final
    parts = [
        ([jnp.concatenate(first, axis=0)], ((0, 2),)),
        ([jnp.concatenate(middle, axis=0)], ((4, 2),)),
        ([near, far], ((20, 2), (20 + near.shape[0], 1))),
    ]
    state = None
    for index, (windows, layout) in enumerate(parts):
        last = index == len(parts) - 1
        state = attend_part(
            info, query_all, windows, layout, low_tile, mean, state, last, queries.shape[1]
        )
    return state


def solution(mesh):
    in_specs = (
        P("seq", "head"),
        P(("seq", "head"), None),
        P(("seq", "head"), None),
        P("seq", "head"),
        P("seq", "head"),
        P("head"),
        P(),
    )
    out_specs = P("seq", "head")
    return jax.shard_map(shards, mesh=mesh, in_specs=in_specs, out_specs=out_specs, check_vma=False)
```

```python
import functools
import math

import jax
import jax.numpy as jnp
from jax import lax
from jax.experimental import pallas as pl
from jax.experimental.pallas import tpu as pltpu
from jax.sharding import PartitionSpec as P

QH = 64
KVH = 8
HD = 128
BLK = 64
MOST = 5120

NEG = -1e30


def doc_index(positions, starts):
    return jnp.sum((starts[None, :] <= positions[:, None]).astype(jnp.int32), axis=1) - 1


def shift_from(x, offset, count):
    pairs = [(i, (i + offset) % count) for i in range(count)]
    return lax.ppermute(x, "seq", pairs)


def gather_stages(packet, count, depth):
    first = [packet[None]] + [shift_from(packet[None], offset, count) for offset in (1, 2, 3)]
    block = jnp.concatenate(first, axis=0)
    middle = [shift_from(block, offset, count) for offset in (4, 8, 12, 16)]
    block = jnp.concatenate([block] + middle, axis=0)
    last = [shift_from(block[4:], 16, count), shift_from(block[4:depth - 32], 32, count)]
    return block, last


def attention_kernel(first, last, layout, *refs):
    count = len(layout)
    info_ref, query_ref = refs[:2]
    windows = refs[2:2 + count]
    low_ref, mean_ref = refs[2 + count:4 + count]
    rest = refs[4 + count:]
    if not first:
        max_in, sum_in, acc_in = rest[:3]
        rest = rest[3:]
    if last:
        out_ref = rest[0]
        rest = rest[1:]
    else:
        max_out, sum_out, acc_out = rest[:3]
        rest = rest[3:]
    max_ref, sum_ref, acc_ref = rest
    group_size, rows = max_ref.shape
    inv_scale = 1.0 / math.sqrt(HD)
    seq_index = info_ref[0]
    used = info_ref[1]
    low_top = info_ref[2]
    if first:
        max_ref[...] = jnp.full(max_ref.shape, NEG, jnp.float32)
        sum_ref[...] = jnp.zeros(sum_ref.shape, jnp.float32)
        acc_ref[...] = jnp.zeros(acc_ref.shape, jnp.float32)
    else:
        max_ref[...] = max_in[...]
        sum_ref[...] = sum_in[...]
        acc_ref[...] = acc_in[...]
    query_pos = seq_index * rows + lax.broadcasted_iota(jnp.int32, (rows, rows), 1)
    low = jnp.broadcast_to(low_ref[0:1, :], (rows, rows))
    sub = lax.broadcasted_iota(jnp.int32, (rows, rows), 0)
    query_t = query_ref[...]

    def column(window_ref, slot, part):
        row = window_ref[slot, part, rows:rows + 1, :].astype(jnp.float32)
        return jnp.transpose(jnp.broadcast_to(row, (rows, rows)))

    def fold_pair(window_ref, offset, step, pair, masked):
        parts = []
        for half in range(step):
            slot = step * pair + half
            key_tile = window_ref[slot, 0, :rows, :]
            scores = jnp.dot(key_tile, query_t, preferred_element_type=jnp.float32)
            key_scale = column(window_ref, slot, 0) * inv_scale
            value_scale = column(window_ref, slot, 1)
            allowed = None
            if masked:
                key_pos = (seq_index - offset - slot) * rows + sub
                allowed = (key_pos <= query_pos) & (key_pos >= low)
            blocks = []
            for g in range(group_size):
                block = scores[:, g * rows:(g + 1) * rows] * key_scale
                if masked:
                    block = jnp.where(allowed, block, NEG)
                blocks.append(block)
            parts.append((blocks, allowed, value_scale, slot))
        for g in range(group_size):
            run_max = max_ref[g:g + 1, :]
            new_max = run_max
            for blocks, _, _, _ in parts:
                new_max = jnp.maximum(new_max, jnp.max(blocks[g], axis=0, keepdims=True))
            factor = jnp.exp(run_max - new_max)
            run_sum = sum_ref[g:g + 1, :] * factor
            acc = acc_ref[:, g * rows:(g + 1) * rows] * factor
            for blocks, allowed, value_scale, slot in parts:
                weights = jnp.exp(blocks[g] - new_max)
                if masked:
                    weights = jnp.where(allowed, weights, 0.0)
                run_sum = run_sum + jnp.sum(weights, axis=0, keepdims=True)
                scaled = (weights * value_scale).astype(jnp.bfloat16)
                value_t = window_ref[slot, 1, :HD, :]
                acc = acc + jnp.dot(value_t, scaled, preferred_element_type=jnp.float32)
            acc_ref[:, g * rows:(g + 1) * rows] = acc
            max_ref[g:g + 1, :] = new_max
            sum_ref[g:g + 1, :] = run_sum

    for window_ref, (offset, step) in zip(windows, layout):

        def one_step(pair, carry, window_ref=window_ref, offset=offset, step=step):
            nearest = offset + step * pair
            inside = (nearest >= 1) & ((seq_index - nearest - step + 1) * rows >= low_top)
            lax.cond(
                inside,
                lambda: fold_pair(window_ref, offset, step, pair, False),
                lambda: fold_pair(window_ref, offset, step, pair, True),
            )
            return carry

        reach = jnp.minimum(jnp.maximum(used - offset, 0), window_ref.shape[0])
        lax.fori_loop(0, (reach + step - 1) // step, one_step, 0)
    if last:
        mean = mean_ref[...]
        for g in range(group_size):
            block = acc_ref[:, g * rows:(g + 1) * rows] / sum_ref[g:g + 1, :] + mean
            out_ref[:, g * HD:(g + 1) * HD] = jnp.transpose(block).astype(jnp.bfloat16)
    else:
        max_out[...] = max_ref[...]
        sum_out[...] = sum_ref[...]
        acc_out[...] = acc_ref[...]


def attend_part(info, query_t, windows, layout, low, mean, state, last, width):
    group_size = query_t.shape[1] // HD
    rows = low.shape[1]
    full = lambda shape: pl.BlockSpec(shape, lambda i, info: (0,) * len(shape))
    row_shape = jax.ShapeDtypeStruct((group_size, rows), jnp.float32)
    acc_shape = jax.ShapeDtypeStruct((HD, group_size * rows), jnp.float32)
    operands = [query_t] + list(windows) + [low, mean] + ([] if state is None else list(state))
    if last:
        out_shape = jax.ShapeDtypeStruct((rows, width), jnp.bfloat16)
        out_specs = full((rows, width))
    else:
        out_shape = (row_shape, row_shape, acc_shape)
        out_specs = (full(row_shape.shape), full(row_shape.shape), full(acc_shape.shape))
    kernel = functools.partial(attention_kernel, state is None, last, layout)
    return pl.pallas_call(
        kernel,
        out_shape=out_shape,
        grid_spec=pltpu.PrefetchScalarGridSpec(
            num_scalar_prefetch=1,
            grid=(1,),
            in_specs=[full(x.shape) for x in operands],
            out_specs=out_specs,
            scratch_shapes=[
                pltpu.VMEM(row_shape.shape, jnp.float32),
                pltpu.VMEM(row_shape.shape, jnp.float32),
                pltpu.VMEM(acc_shape.shape, jnp.float32),
            ],
        ),
    )(info, *operands)


def shards(queries, key_tokens, value_tokens, key_scales, value_scales, value_means, doc_lengths):
    heads = lax.axis_size("head")
    rows_in = key_tokens.shape[0]
    both = jnp.concatenate([key_tokens, value_tokens], axis=0)
    both = lax.all_to_all(both, "head", split_axis=1, concat_axis=0, tiled=True)
    both = both.reshape(heads, 2, rows_in, HD)
    local_keys = both[:, 0].reshape(heads * rows_in, HD)
    local_values = both[:, 1].reshape(heads * rows_in, HD)
    row_count = local_keys.shape[0]
    group_size = QH // KVH
    seq_count = lax.axis_size("seq")
    seq_index = lax.axis_index("seq")
    starts = jnp.cumsum(doc_lengths) - doc_lengths
    depth = min(seq_count, -(-(MOST - 1) // row_count) + 1)
    pad_rows = 8
    key_scale_row = jnp.repeat(key_scales.reshape(-1), BLK)
    value_scale_row = jnp.repeat(value_scales.reshape(-1), BLK)
    scale_rows = jnp.zeros((2, pad_rows, row_count), jnp.bfloat16)
    scale_rows = scale_rows.at[0, 0].set(key_scale_row).at[1, 0].set(value_scale_row)
    packet = jnp.concatenate([jnp.stack([local_keys, local_values.T]), scale_rows], axis=1)
    stages = gather_stages(packet, seq_count, depth)
    own_pos = seq_index * row_count + jnp.arange(row_count, dtype=jnp.int32)
    low = starts[doc_index(own_pos, starts)]
    used = jnp.clip(seq_index - low[0] // row_count + 1, 1, depth).astype(jnp.int32)
    low_tile = jnp.broadcast_to(low[None, :], (8, row_count)).astype(jnp.int32)
    mean = jnp.broadcast_to(value_means.reshape(HD, 1), (HD, row_count))
    query_all = queries.reshape(row_count, group_size, HD).transpose(2, 1, 0).reshape(HD, -1)
    info = jnp.stack([seq_index.astype(jnp.int32), used, low[-1].astype(jnp.int32)])
    block, (near, far) = stages
    parts = [
        ([block], ((0, 2),)),
        ([near, far], ((block.shape[0], 2), (block.shape[0] + near.shape[0], 1))),
    ]
    state = None
    for index, (windows, layout) in enumerate(parts):
        last = index == len(parts) - 1
        state = attend_part(
            info, query_all, windows, layout, low_tile, mean, state, last, queries.shape[1]
        )
    return state


def solution(mesh):
    in_specs = (
        P("seq", "head"),
        P(("seq", "head"), None),
        P(("seq", "head"), None),
        P("seq", "head"),
        P("seq", "head"),
        P("head"),
        P(),
    )
    out_specs = P("seq", "head")
    return jax.shard_map(shards, mesh=mesh, in_specs=in_specs, out_specs=out_specs, check_vma=False)
```

```python
import functools
import math

import jax
import jax.numpy as jnp
from jax import lax
from jax.experimental import pallas as pl
from jax.experimental.pallas import tpu as pltpu
from jax.sharding import PartitionSpec as P

QH = 64
KVH = 8
HD = 128
BLK = 64
MOST = 5120

NEG = -1e30


def doc_index(positions, starts):
    return jnp.sum((starts[None, :] <= positions[:, None]).astype(jnp.int32), axis=1) - 1


def shift_from(x, offset, count):
    pairs = [(i, (i + offset) % count) for i in range(count)]
    return lax.ppermute(x, "seq", pairs)


def gather_stages(packet, count, depth):
    first = [packet[None]] + [shift_from(packet[None], offset, count) for offset in (1, 2, 3)]
    block = jnp.concatenate(first, axis=0)
    middle = [shift_from(block, offset, count) for offset in (4, 8, 12, 16)]
    block = jnp.concatenate([block] + middle, axis=0)
    last = [shift_from(block[4:], 16, count), shift_from(block[4:depth - 32], 32, count)]
    return [first, middle, last]


def attention_kernel(first, last, layout, *refs):
    count = len(layout)
    info_ref, query_ref = refs[:2]
    windows = refs[2:2 + count]
    low_ref, mean_ref = refs[2 + count:4 + count]
    rest = refs[4 + count:]
    if not first:
        max_in, sum_in, acc_in = rest[:3]
        rest = rest[3:]
    if last:
        out_ref = rest[0]
        rest = rest[1:]
    else:
        max_out, sum_out, acc_out = rest[:3]
        rest = rest[3:]
    max_ref, sum_ref, acc_ref = rest
    group_size, rows = max_ref.shape
    inv_scale = 1.0 / math.sqrt(HD)
    seq_index = info_ref[0]
    used = info_ref[1]
    low_top = info_ref[2]
    if first:
        max_ref[...] = jnp.full(max_ref.shape, NEG, jnp.float32)
        sum_ref[...] = jnp.zeros(sum_ref.shape, jnp.float32)
        acc_ref[...] = jnp.zeros(acc_ref.shape, jnp.float32)
    else:
        max_ref[...] = max_in[...]
        sum_ref[...] = sum_in[...]
        acc_ref[...] = acc_in[...]
    query_pos = seq_index * rows + lax.broadcasted_iota(jnp.int32, (rows, rows), 1)
    low = jnp.broadcast_to(low_ref[0:1, :], (rows, rows))
    sub = lax.broadcasted_iota(jnp.int32, (rows, rows), 0)
    query_t = query_ref[...]

    def column(window_ref, slot, part):
        row = window_ref[slot, part, rows:rows + 1, :].astype(jnp.float32)
        return jnp.transpose(jnp.broadcast_to(row, (rows, rows)))

    def fold_pair(window_ref, offset, step, pair, masked):
        parts = []
        for half in range(step):
            slot = step * pair + half
            key_tile = window_ref[slot, 0, :rows, :]
            scores = jnp.dot(key_tile, query_t, preferred_element_type=jnp.float32)
            key_scale = column(window_ref, slot, 0) * inv_scale
            value_scale = column(window_ref, slot, 1)
            allowed = None
            if masked:
                key_pos = (seq_index - offset - slot) * rows + sub
                allowed = (key_pos <= query_pos) & (key_pos >= low)
            blocks = []
            for g in range(group_size):
                block = scores[:, g * rows:(g + 1) * rows] * key_scale
                if masked:
                    block = jnp.where(allowed, block, NEG)
                blocks.append(block)
            parts.append((blocks, allowed, value_scale, slot))
        for g in range(group_size):
            run_max = max_ref[g:g + 1, :]
            new_max = run_max
            for blocks, _, _, _ in parts:
                new_max = jnp.maximum(new_max, jnp.max(blocks[g], axis=0, keepdims=True))
            factor = jnp.exp(run_max - new_max)
            run_sum = sum_ref[g:g + 1, :] * factor
            acc = acc_ref[:, g * rows:(g + 1) * rows] * factor
            for blocks, allowed, value_scale, slot in parts:
                weights = jnp.exp(blocks[g] - new_max)
                if masked:
                    weights = jnp.where(allowed, weights, 0.0)
                run_sum = run_sum + jnp.sum(weights, axis=0, keepdims=True)
                scaled = (weights * value_scale).astype(jnp.bfloat16)
                value_t = window_ref[slot, 1, :HD, :]
                acc = acc + jnp.dot(value_t, scaled, preferred_element_type=jnp.float32)
            acc_ref[:, g * rows:(g + 1) * rows] = acc
            max_ref[g:g + 1, :] = new_max
            sum_ref[g:g + 1, :] = run_sum

    for window_ref, (offset, step) in zip(windows, layout):

        def one_step(pair, carry, window_ref=window_ref, offset=offset, step=step):
            nearest = offset + step * pair
            inside = (nearest >= 1) & ((seq_index - nearest - step + 1) * rows >= low_top)
            lax.cond(
                inside,
                lambda: fold_pair(window_ref, offset, step, pair, False),
                lambda: fold_pair(window_ref, offset, step, pair, True),
            )
            return carry

        reach = jnp.minimum(jnp.maximum(used - offset, 0), window_ref.shape[0])
        lax.fori_loop(0, (reach + step - 1) // step, one_step, 0)
    if last:
        mean = mean_ref[...]
        for g in range(group_size):
            block = acc_ref[:, g * rows:(g + 1) * rows] / sum_ref[g:g + 1, :] + mean
            out_ref[:, g * HD:(g + 1) * HD] = jnp.transpose(block).astype(jnp.bfloat16)
    else:
        max_out[...] = max_ref[...]
        sum_out[...] = sum_ref[...]
        acc_out[...] = acc_ref[...]


def attend_part(info, query_t, windows, layout, low, mean, state, last, width):
    group_size = query_t.shape[1] // HD
    rows = low.shape[1]
    full = lambda shape: pl.BlockSpec(shape, lambda i, info: (0,) * len(shape))
    row_shape = jax.ShapeDtypeStruct((group_size, rows), jnp.float32)
    acc_shape = jax.ShapeDtypeStruct((HD, group_size * rows), jnp.float32)
    operands = [query_t] + list(windows) + [low, mean] + ([] if state is None else list(state))
    if last:
        out_shape = jax.ShapeDtypeStruct((rows, width), jnp.bfloat16)
        out_specs = full((rows, width))
    else:
        out_shape = (row_shape, row_shape, acc_shape)
        out_specs = (full(row_shape.shape), full(row_shape.shape), full(acc_shape.shape))
    kernel = functools.partial(attention_kernel, state is None, last, layout)
    return pl.pallas_call(
        kernel,
        out_shape=out_shape,
        grid_spec=pltpu.PrefetchScalarGridSpec(
            num_scalar_prefetch=1,
            grid=(1,),
            in_specs=[full(x.shape) for x in operands],
            out_specs=out_specs,
            scratch_shapes=[
                pltpu.VMEM(row_shape.shape, jnp.float32),
                pltpu.VMEM(row_shape.shape, jnp.float32),
                pltpu.VMEM(acc_shape.shape, jnp.float32),
            ],
        ),
    )(info, *operands)


def shards(queries, key_tokens, value_tokens, key_scales, value_scales, value_means, doc_lengths):
    heads = lax.axis_size("head")
    rows_in = key_tokens.shape[0]
    both = jnp.concatenate([key_tokens, value_tokens], axis=0)
    both = lax.all_to_all(both, "head", split_axis=1, concat_axis=0, tiled=True)
    both = both.reshape(heads, 2, rows_in, HD)
    local_keys = both[:, 0].reshape(heads * rows_in, HD)
    local_values = both[:, 1].reshape(heads * rows_in, HD)
    row_count = local_keys.shape[0]
    group_size = QH // KVH
    seq_count = lax.axis_size("seq")
    seq_index = lax.axis_index("seq")
    starts = jnp.cumsum(doc_lengths) - doc_lengths
    depth = min(seq_count, -(-(MOST - 1) // row_count) + 1)
    pad_rows = 8
    key_scale_row = jnp.repeat(key_scales.reshape(-1), BLK)
    value_scale_row = jnp.repeat(value_scales.reshape(-1), BLK)
    scale_rows = jnp.zeros((2, pad_rows, row_count), jnp.bfloat16)
    scale_rows = scale_rows.at[0, 0].set(key_scale_row).at[1, 0].set(value_scale_row)
    packet = jnp.concatenate([jnp.stack([local_keys, local_values.T]), scale_rows], axis=1)
    stages = gather_stages(packet, seq_count, depth)
    own_pos = seq_index * row_count + jnp.arange(row_count, dtype=jnp.int32)
    low = starts[doc_index(own_pos, starts)]
    used = jnp.clip(seq_index - low[0] // row_count + 1, 1, depth).astype(jnp.int32)
    low_tile = jnp.broadcast_to(low[None, :], (8, row_count)).astype(jnp.int32)
    mean = jnp.broadcast_to(value_means.reshape(HD, 1), (HD, row_count))
    query_all = queries.reshape(row_count, group_size, HD).transpose(2, 1, 0).reshape(HD, -1)
    info = jnp.stack([seq_index.astype(jnp.int32), used, low[-1].astype(jnp.int32)])
    first, middle, final = stages
    near, far = final
    parts = [
        ([jnp.concatenate(first, axis=0)], ((0, 2),)),
        (middle, tuple((4 * (index + 1), 2) for index in range(len(middle)))),
        ([near, far], ((20, 2), (20 + near.shape[0], 1))),
    ]
    state = None
    for index, (windows, layout) in enumerate(parts):
        last = index == len(parts) - 1
        state = attend_part(
            info, query_all, windows, layout, low_tile, mean, state, last, queries.shape[1]
        )
    return state


def solution(mesh):
    in_specs = (
        P("seq", "head"),
        P(("seq", "head"), None),
        P(("seq", "head"), None),
        P("seq", "head"),
        P("seq", "head"),
        P("head"),
        P(),
    )
    out_specs = P("seq", "head")
    return jax.shard_map(shards, mesh=mesh, in_specs=in_specs, out_specs=out_specs, check_vma=False)
```

```python
import functools
import math

import jax
import jax.numpy as jnp
from jax import lax
from jax.experimental import pallas as pl
from jax.experimental.pallas import tpu as pltpu
from jax.sharding import PartitionSpec as P

QH = 64
KVH = 8
HD = 128
BLK = 64
MOST = 5120

NEG = -1e30


def doc_index(positions, starts):
    return jnp.sum((starts[None, :] <= positions[:, None]).astype(jnp.int32), axis=1) - 1


def shift_from(x, offset, count):
    pairs = [(i, (i + offset) % count) for i in range(count)]
    return lax.ppermute(x, "seq", pairs)


def gather_stages(packet, count, depth):
    first = [packet[None]] + [shift_from(packet[None], offset, count) for offset in (1, 2, 3)]
    block = jnp.concatenate(first, axis=0)
    middle = [shift_from(block, offset, count) for offset in (4, 8, 12, 16)]
    block = jnp.concatenate([block] + middle, axis=0)
    last = [shift_from(block[4:], 16, count), shift_from(block[4:depth - 32], 32, count)]
    return [first, middle, last]


def attention_kernel(first, last, layout, *refs):
    count = len(layout)
    info_ref, query_ref = refs[:2]
    windows = refs[2:2 + count]
    low_ref, mean_ref = refs[2 + count:4 + count]
    rest = refs[4 + count:]
    if not first:
        max_in, sum_in, acc_in = rest[:3]
        rest = rest[3:]
    if last:
        out_ref = rest[0]
        rest = rest[1:]
    else:
        max_out, sum_out, acc_out = rest[:3]
        rest = rest[3:]
    max_ref, sum_ref, acc_ref = rest
    group_size, rows = max_ref.shape
    inv_scale = 1.0 / math.sqrt(HD)
    seq_index = info_ref[0]
    used = info_ref[1]
    low_top = info_ref[2]
    if first:
        max_ref[...] = jnp.full(max_ref.shape, NEG, jnp.float32)
        sum_ref[...] = jnp.zeros(sum_ref.shape, jnp.float32)
        acc_ref[...] = jnp.zeros(acc_ref.shape, jnp.float32)
    else:
        max_ref[...] = max_in[...]
        sum_ref[...] = sum_in[...]
        acc_ref[...] = acc_in[...]
    query_pos = seq_index * rows + lax.broadcasted_iota(jnp.int32, (rows, rows), 1)
    low = jnp.broadcast_to(low_ref[0:1, :], (rows, rows))
    sub = lax.broadcasted_iota(jnp.int32, (rows, rows), 0)
    query_t = query_ref[...]

    def column(window_ref, slot, part):
        row = window_ref[slot, part, rows:rows + 1, :].astype(jnp.float32)
        return jnp.transpose(jnp.broadcast_to(row, (rows, rows)))

    def fold_pair(window_ref, offset, step, begin, pair, masked):
        parts = []
        for half in range(step):
            slot = begin + step * pair + half
            key_tile = window_ref[slot, 0, :rows, :]
            scores = jnp.dot(key_tile, query_t, preferred_element_type=jnp.float32)
            key_scale = column(window_ref, slot, 0) * inv_scale
            value_scale = column(window_ref, slot, 1)
            allowed = None
            if masked:
                key_pos = (seq_index - offset - slot) * rows + sub
                allowed = (key_pos <= query_pos) & (key_pos >= low)
            blocks = []
            for g in range(group_size):
                block = scores[:, g * rows:(g + 1) * rows] * key_scale
                if masked:
                    block = jnp.where(allowed, block, NEG)
                blocks.append(block)
            parts.append((blocks, allowed, value_scale, slot))
        for g in range(group_size):
            run_max = max_ref[g:g + 1, :]
            new_max = run_max
            for blocks, _, _, _ in parts:
                new_max = jnp.maximum(new_max, jnp.max(blocks[g], axis=0, keepdims=True))
            factor = jnp.exp(run_max - new_max)
            run_sum = sum_ref[g:g + 1, :] * factor
            acc = acc_ref[:, g * rows:(g + 1) * rows] * factor
            for blocks, allowed, value_scale, slot in parts:
                weights = jnp.exp(blocks[g] - new_max)
                if masked:
                    weights = jnp.where(allowed, weights, 0.0)
                run_sum = run_sum + jnp.sum(weights, axis=0, keepdims=True)
                scaled = (weights * value_scale).astype(jnp.bfloat16)
                value_t = window_ref[slot, 1, :HD, :]
                acc = acc + jnp.dot(value_t, scaled, preferred_element_type=jnp.float32)
            acc_ref[:, g * rows:(g + 1) * rows] = acc
            max_ref[g:g + 1, :] = new_max
            sum_ref[g:g + 1, :] = run_sum

    for window_ref, (offset, step, begin, end) in zip(windows, layout):

        def one_step(pair, carry, window_ref=window_ref, offset=offset, step=step, begin=begin):
            nearest = offset + begin + step * pair
            inside = (nearest >= 1) & ((seq_index - nearest - step + 1) * rows >= low_top)
            lax.cond(
                inside,
                lambda: fold_pair(window_ref, offset, step, begin, pair, False),
                lambda: fold_pair(window_ref, offset, step, begin, pair, True),
            )
            return carry

        reach = jnp.minimum(jnp.maximum(used - offset - begin, 0), end - begin)
        lax.fori_loop(0, (reach + step - 1) // step, one_step, 0)
    if last:
        mean = mean_ref[...]
        for g in range(group_size):
            block = acc_ref[:, g * rows:(g + 1) * rows] / sum_ref[g:g + 1, :] + mean
            out_ref[:, g * HD:(g + 1) * HD] = jnp.transpose(block).astype(jnp.bfloat16)
    else:
        max_out[...] = max_ref[...]
        sum_out[...] = sum_ref[...]
        acc_out[...] = acc_ref[...]


def attend_part(info, query_t, windows, layout, low, mean, state, last, width):
    group_size = query_t.shape[1] // HD
    rows = low.shape[1]
    full = lambda shape: pl.BlockSpec(shape, lambda i, info: (0,) * len(shape))
    row_shape = jax.ShapeDtypeStruct((group_size, rows), jnp.float32)
    acc_shape = jax.ShapeDtypeStruct((HD, group_size * rows), jnp.float32)
    operands = [query_t] + list(windows) + [low, mean] + ([] if state is None else list(state))
    if last:
        out_shape = jax.ShapeDtypeStruct((rows, width), jnp.bfloat16)
        out_specs = full((rows, width))
    else:
        out_shape = (row_shape, row_shape, acc_shape)
        out_specs = (full(row_shape.shape), full(row_shape.shape), full(acc_shape.shape))
    kernel = functools.partial(attention_kernel, state is None, last, layout)
    return pl.pallas_call(
        kernel,
        out_shape=out_shape,
        grid_spec=pltpu.PrefetchScalarGridSpec(
            num_scalar_prefetch=1,
            grid=(1,),
            in_specs=[full(x.shape) for x in operands],
            out_specs=out_specs,
            scratch_shapes=[
                pltpu.VMEM(row_shape.shape, jnp.float32),
                pltpu.VMEM(row_shape.shape, jnp.float32),
                pltpu.VMEM(acc_shape.shape, jnp.float32),
            ],
        ),
    )(info, *operands)


def shards(queries, key_tokens, value_tokens, key_scales, value_scales, value_means, doc_lengths):
    heads = lax.axis_size("head")
    rows_in = key_tokens.shape[0]
    both = jnp.concatenate([key_tokens, value_tokens], axis=0)
    both = lax.all_to_all(both, "head", split_axis=1, concat_axis=0, tiled=True)
    both = both.reshape(heads, 2, rows_in, HD)
    local_keys = both[:, 0].reshape(heads * rows_in, HD)
    local_values = both[:, 1].reshape(heads * rows_in, HD)
    row_count = local_keys.shape[0]
    group_size = QH // KVH
    seq_count = lax.axis_size("seq")
    seq_index = lax.axis_index("seq")
    starts = jnp.cumsum(doc_lengths) - doc_lengths
    depth = min(seq_count, -(-(MOST - 1) // row_count) + 1)
    pad_rows = 8
    key_scale_row = jnp.repeat(key_scales.reshape(-1), BLK)
    value_scale_row = jnp.repeat(value_scales.reshape(-1), BLK)
    scale_rows = jnp.zeros((2, pad_rows, row_count), jnp.bfloat16)
    scale_rows = scale_rows.at[0, 0].set(key_scale_row).at[1, 0].set(value_scale_row)
    packet = jnp.concatenate([jnp.stack([local_keys, local_values.T]), scale_rows], axis=1)
    stages = gather_stages(packet, seq_count, depth)
    own_pos = seq_index * row_count + jnp.arange(row_count, dtype=jnp.int32)
    low = starts[doc_index(own_pos, starts)]
    used = jnp.clip(seq_index - low[0] // row_count + 1, 1, depth).astype(jnp.int32)
    low_tile = jnp.broadcast_to(low[None, :], (8, row_count)).astype(jnp.int32)
    mean = jnp.broadcast_to(value_means.reshape(HD, 1), (HD, row_count))
    query_all = queries.reshape(row_count, group_size, HD).transpose(2, 1, 0).reshape(HD, -1)
    info = jnp.stack([seq_index.astype(jnp.int32), used, low[-1].astype(jnp.int32)])
    first, middle, final = stages
    near, far = final
    parts = [
        ([jnp.concatenate(first, axis=0)], ((0, 2, 0, 4),)),
        ([jnp.concatenate(middle, axis=0)], ((4, 2, 0, 16),)),
        (
            [near, far, far],
            ((20, 2, 0, 16), (36, 2, 0, far.shape[0] - 1), (36, 1, far.shape[0] - 1, far.shape[0])),
        ),
    ]
    state = None
    for index, (windows, layout) in enumerate(parts):
        last = index == len(parts) - 1
        state = attend_part(
            info, query_all, windows, layout, low_tile, mean, state, last, queries.shape[1]
        )
    return state


def solution(mesh):
    in_specs = (
        P("seq", "head"),
        P(("seq", "head"), None),
        P(("seq", "head"), None),
        P("seq", "head"),
        P("seq", "head"),
        P("head"),
        P(),
    )
    out_specs = P("seq", "head")
    return jax.shard_map(shards, mesh=mesh, in_specs=in_specs, out_specs=out_specs, check_vma=False)
```
